512 devices in a mesh: seq: 128 (over x, z, core), head: 4 (over y).
Axes of the slice: x: 4, y: 4, z: 16, core: 2. Of those that a mesh axis runs over, the one named last changes fastest.
Arguments:
- hidden: bfloat16 [32768, 2560], P(('seq', 'head')), may hold values from -6 to 6
- w_values: bfloat16 [2560, 2560], P('seq', 'head'), may hold values from -0.125 to 0.125
- w_gates: bfloat16 [2560, 2560], P('seq', 'head'), may hold values from -0.125 to 0.125
- w_steps: bfloat16 [2560, 40], P('seq', 'head'), may hold values from -0.0625 to 0.0625
- w_states: bfloat16 [2560, 256], P('seq'), may hold values from -0.125 to 0.125
- conv_weight: float32 [4, 2816], replicated, may hold values from -3 to 3
- conv_bias: float32 [2816], replicated, may hold values from -3 to 3
- step_bias: float32 [40], P('head'), may hold values from -1 to 0.5
- decay_rate: float32 [40], P('head'), may hold values from 0 to 1, as said below
- skip_gain: float32 [40], P('head'), may hold values from 1 to 8
- norm_gain: float32 [2560], replicated, may hold values from 0.5 to 1.5
- lengths: int32 [64], replicated, may hold values from 256 to 768, as said below
Outputs:
- gated_out: bfloat16 [32768, 2560], P(('seq', 'head'))
- final_states: float32 [128, 40, 64, 128], P('seq', 'head')
The draws below stay inside these ranges and needn't reach their ends.
Inputs may be any that keep to these rules, and one draw needn't show every extreme that they name: Prompts are packed in order, each holding 256 to 768 tokens; the lengths sum to 32768. `decay_rate`: positive rates.
All inputs are finite; a program needn't handle non-finite values.
Results may differ from the reference program's by a relative error of at most 0.01.
Values may be sent and summed in bfloat16 or wider, within the bound.
No kernel may reach another device: no remote copies, remote signals or barrier semaphores. Data moves between devices by JAX's collectives and lax.ppermute only.
A program may use at most 128 MiB of HBM per device.

```python
import math
import jax
import jax.numpy as jnp
from jax import lax

D = 2560
HEADS = 40
HEAD_DIM = 64
STATE = 128
CONV = 4
STRETCH = 256
TOK_DEV = 256
INNER = 2560
CONV_CH = 2816
TOKENS = 32768
BLOCKS = 128
PROMPTS = 64


def draw_lengths(key, part):
    order_key = jax.random.fold_in(key, 11)
    offset_key = jax.random.fold_in(key, 12)
    cycle_order = jax.random.permutation(order_key, PROMPTS)
    offsets = jax.random.randint(offset_key, (PROMPTS,), 0, TOK_DEV + 1)
    cycle_slots = jnp.arange(PROMPTS, dtype=jnp.int32)
    offsets = jnp.where(cycle_slots == 0, TOK_DEV, offsets)
    offsets = jnp.where(cycle_slots == 1, 0, offsets)
    offsets = jnp.where(cycle_slots == 2, TOK_DEV, offsets)
    along_cycle = 2 * TOK_DEV + offsets - jnp.roll(offsets, -1)
    placing = jnp.argsort(cycle_order, stable=True)
    return along_cycle[placing].astype(jnp.int32)


def draw_decay_rate(key, part):
    pick_key = jax.random.fold_in(key, 21)
    slow_key = jax.random.fold_in(key, 22)
    fast_key = jax.random.fold_in(key, 23)
    chooser = jax.random.uniform(pick_key, (HEADS,), jnp.float32)
    fast_share = 0.5
    slow_rate = jnp.exp(jax.random.uniform(slow_key, (HEADS,), jnp.float32, math.log(0.1), math.log(0.8))) / (3.0 * TOK_DEV)
    fast_rate = jnp.exp(jax.random.uniform(fast_key, (HEADS,), jnp.float32, math.log(0.04), math.log(0.12)))
    return jnp.where(chooser < fast_share, fast_rate, slow_rate).astype(jnp.float32)


def block_scale(rng, shape, split, low, largest):
    gain = 1.0
    for dim, parts in split:
        heights = jax.random.uniform(jax.random.fold_in(jax.random.fold_in(rng, 6), dim), (parts,), jnp.float32, low / len(split), largest / len(split))
        gain = gain * jnp.repeat(jnp.exp(heights), shape[dim] // parts).reshape((-1,) + (1,) * (len(shape) - 1 - dim))
    return gain


def centred(own_key, extent, width, most, split=(), kind=jnp.bfloat16):
    entries = jax.random.normal(own_key, extent, jnp.float32) * width
    if len(split) > 0:
        entries = block_scale(own_key, extent, split, -0.22, 0.18) * entries
    return jnp.clip(entries, min=-most, max=most).astype(kind)


def setup_inputs(seed: int = 0) -> dict:
    key_of = jax.random.split(jax.random.key(seed), 13)
    hidden = centred(key_of[0], (TOKENS, D), 1.0, 6.0, ((0, 512),))
    w_values = centred(key_of[1], (D, INNER), D ** -0.5, 0.125, ((0, 128), (1, 4)))
    w_gates = centred(key_of[2], (D, INNER), D ** -0.5, 0.125, ((0, 128), (1, 4)))
    w_steps = centred(key_of[3], (D, HEADS), (4 * D) ** -0.5, 0.0625, ((0, 128), (1, 4)))
    w_states = centred(key_of[4], (D, 2 * STATE), D ** -0.5, 0.125, ((0, 128),))
    conv_weight = centred(key_of[5], (CONV, CONV_CH), CONV ** -0.5, 3.0, (), jnp.float32)
    conv_bias = centred(key_of[6], (CONV_CH,), 0.5, 3.0, (), jnp.float32)
    step_bias = jnp.clip(-1.0 + 1.5 * jax.random.uniform(key_of[7], (HEADS,), jnp.float32) ** block_scale(key_of[7], (HEADS,), ((0, 4),), -0.2, 0.2), -1.0, 0.5)
    decay_rate = draw_decay_rate(jax.random.fold_in(key_of[12], 71), 0)
    skip_gain = jnp.clip(1.0 + 7.0 * jax.random.uniform(key_of[9], (HEADS,), jnp.float32) ** block_scale(key_of[9], (HEADS,), ((0, 4),), -0.2, 0.2), 1.0, 8.0)
    norm_gain = jnp.clip(1.0 + 0.1 * jax.random.normal(key_of[10], (INNER,), jnp.float32), 0.5, 1.5)
    lengths = draw_lengths(jax.random.fold_in(key_of[12], 71), 0)
    return {"hidden": hidden, "w_values": w_values, "w_gates": w_gates, "w_steps": w_steps, "w_states": w_states, "conv_weight": conv_weight, "conv_bias": conv_bias, "step_bias": step_bias, "decay_rate": decay_rate, "skip_gain": skip_gain, "norm_gain": norm_gain, "lengths": lengths}


epsilon = 1e-05
highest = lax.Precision.HIGHEST

def segments_at(positions, prompt_ends):
    counted = lax.optimization_barrier(jnp.sum((prompt_ends[None, :] <= positions[:, None]).astype(jnp.int32), axis=1)).astype(jnp.int32)
    return jnp.where(positions < 0, -1, counted).astype(jnp.int32)

def rounded(values):
    return lax.optimization_barrier(values.astype(jnp.bfloat16)).astype(jnp.float32)

def stretch_pass(skip_gain, running, pieces):
    values, write_state, read_state, step_sizes, decay_steps, stretch_ids, prior_id, ends_mask = pieces
    log_decay = -jnp.cumsum(decay_steps, axis=0)
    decay_heads = log_decay.T
    step_heads = step_sizes.T
    intersection = jnp.dot(read_state, write_state.T, preferred_element_type=jnp.float32)
    positions = jnp.arange(STRETCH, dtype=jnp.int32)
    causal = positions[:, None] >= positions[None, :]
    allowed = causal & (stretch_ids[:, None] == stretch_ids[None, :])
    spread = decay_heads[:, :, None] - decay_heads[:, None, :]
    weights = jnp.where(allowed[None], jnp.exp(jnp.minimum(spread, 0.0)), 0.0) * step_heads[:, None, :]
    scores = rounded(intersection[None] * weights)
    values_wide = values.astype(jnp.float32)
    within_stretch = jnp.einsum('hts,shp->thp', scores, values_wide, precision=highest)
    last_id = stretch_ids[-1]
    tail_coef = jnp.where((stretch_ids == last_id)[None, :], jnp.exp(jnp.minimum(decay_heads[:, -1:] - decay_heads, 0.0)), 0.0) * step_heads
    tail_rows = rounded(values_wide * tail_coef.T[:, :, None])
    write_wide = write_state.astype(jnp.float32)
    stretch_state = jnp.einsum('lhp,ln->hpn', tail_rows, write_wide, precision=highest)
    stretch_gate = jnp.exp(decay_heads[:, -1]) * (last_id == prior_id).astype(jnp.float32)
    carry_decay = jnp.exp(log_decay) * (stretch_ids == prior_id).astype(jnp.float32)[:, None]
    from_before = jnp.einsum('ln,hpn->lhp', read_state.astype(jnp.float32), rounded(running), precision=highest) * carry_decay[:, :, None]
    result = within_stretch + from_before + skip_gain[None, :, None] * values_wide
    ssm_rows = result.reshape(STRETCH, INNER).astype(jnp.bfloat16)
    end_weight = ends_mask.astype(jnp.float32)
    has_end = jnp.sum(end_weight)
    end_decay = lax.optimization_barrier(jnp.sum(decay_heads * end_weight[None, :], axis=1))
    end_id = jnp.sum(jnp.where(ends_mask, stretch_ids, 0)).astype(jnp.int32)
    keep_end = (stretch_ids == end_id) & (has_end > 0)
    end_coef = jnp.where(keep_end[None, :], jnp.exp(jnp.minimum(end_decay[:, None] - decay_heads, 0.0)), 0.0) * step_heads
    end_rows = rounded(values_wide * end_coef.T[:, :, None])
    end_state = jnp.einsum('lhp,ln->hpn', end_rows, write_wide, precision=highest)
    end_carry = jnp.exp(end_decay) * ((end_id == prior_id) & (has_end > 0)).astype(jnp.float32)
    end_state = end_state + end_carry[:, None, None] * running
    new_running = stretch_gate[:, None, None] * running + stretch_state
    return (new_running, (ssm_rows, end_state))

def partial_pass(skip_gain):

    def stepper(running, pieces):
        return stretch_pass(skip_gain, running, pieces)
    return stepper

def reference(hidden, w_values, w_gates, w_steps, w_states, conv_weight, conv_bias, step_bias, decay_rate, skip_gain, norm_gain, lengths):
    conv_input = jnp.dot(hidden, jnp.concatenate([w_values, w_states], axis=1), preferred_element_type=jnp.float32).astype(jnp.bfloat16)
    gate_input = jnp.dot(hidden, w_gates, preferred_element_type=jnp.float32).astype(jnp.bfloat16)
    step_input = jnp.dot(hidden, w_steps, preferred_element_type=jnp.float32)
    prompt_ends = jnp.cumsum(lengths).astype(jnp.int32)
    positions = jnp.arange(TOKENS, dtype=jnp.int32)
    segment_ids = segments_at(positions, prompt_ends)
    extended = jnp.concatenate([jnp.zeros((CONV - 1, CONV_CH), jnp.bfloat16), conv_input], axis=0)
    ext_ids = jnp.concatenate([jnp.full((CONV - 1,), -1, jnp.int32), segment_ids], axis=0)
    filtered = jnp.zeros((TOKENS, CONV_CH), jnp.float32) + conv_bias[None, :]
    for offset in range(CONV):
        matches = (ext_ids[offset:offset + TOKENS] == segment_ids).astype(jnp.float32)
        filtered = filtered + conv_weight[offset][None, :] * extended[offset:offset + TOKENS].astype(jnp.float32) * matches[:, None]
    conv_out = jax.nn.silu(filtered).astype(jnp.bfloat16)
    stretch_count = TOKENS // STRETCH
    values = conv_out[:, :INNER].reshape(stretch_count, STRETCH, HEADS, HEAD_DIM)
    write_state = conv_out[:, INNER:INNER + STATE].reshape(stretch_count, STRETCH, STATE)
    read_state = conv_out[:, INNER + STATE:].reshape(stretch_count, STRETCH, STATE)
    step_sizes = jax.nn.softplus(step_input + step_bias[None, :])
    decay_steps = step_sizes * decay_rate[None, :]
    before_ids = segments_at(positions - 1, prompt_ends)
    next_ids = segments_at(positions + 1, prompt_ends)
    ends_mask = segment_ids != next_ids
    pieces = (values, write_state, read_state, step_sizes.reshape(stretch_count, STRETCH, HEADS), decay_steps.reshape(stretch_count, STRETCH, HEADS), segment_ids.reshape(stretch_count, STRETCH), before_ids.reshape(stretch_count, STRETCH)[:, 0], ends_mask.reshape(stretch_count, STRETCH))
    start_state = jnp.zeros((HEADS, HEAD_DIM, STATE), jnp.float32)
    final_running, stacked = lax.scan(partial_pass(skip_gain), start_state, pieces)
    ssm_rows = stacked[0].reshape(TOKENS, INNER)
    final_states = lax.optimization_barrier(jnp.sum(stacked[1].reshape(BLOCKS, TOK_DEV // STRETCH, HEADS, HEAD_DIM, STATE), axis=1))
    gated = ssm_rows.astype(jnp.float32) * jax.nn.silu(gate_input.astype(jnp.float32))
    mean_square = lax.optimization_barrier(jnp.mean(gated * gated, axis=1))
    gated_out = (gated * lax.rsqrt(mean_square + epsilon)[:, None] * norm_gain[None, :]).astype(jnp.bfloat16)
    return (gated_out, final_states)
```

```python
import jax
import jax.numpy as jnp
from jax import lax
from jax.sharding import PartitionSpec as P

STRETCH = 256


epsilon = 1e-05


def from_behind(block, axis, distance):
    devices = range(lax.axis_size(axis))
    route = [(i - distance, i) for i in devices if i - distance in devices]
    return lax.ppermute(block, axis, route)


def segments_at(positions, prompt_ends):
    counted = jnp.sum((prompt_ends[None, :] <= positions[:, None]).astype(jnp.int32), axis=1)
    return jnp.where(positions < 0, -1, counted)


def on_device(
    hidden,
    w_values,
    w_gates,
    w_steps,
    w_states,
    conv_weight,
    conv_bias,
    step_bias,
    decay_rate,
    skip_gain,
    norm_gain,
    lengths,
):
    groups = lax.axis_size("head")
    group_index = lax.axis_index("head")
    block_index = lax.axis_index("seq")
    local_width = w_values.shape[1]
    inner_width = local_width * groups
    local_heads = decay_rate.shape[0]
    head_width = local_width // local_heads
    state_width = w_states.shape[1] // 2
    conv_taps = conv_weight.shape[0]
    prompt_ends = jnp.cumsum(lengths)
    block_hidden = lax.all_to_all(
        jnp.broadcast_to(hidden[None], (groups,) + hidden.shape), "head", 0, 0, tiled=True
    ).reshape(groups * hidden.shape[0], hidden.shape[1])
    block_rows = block_hidden.shape[0]
    sub_rows = block_rows // groups
    step_width = w_steps.shape[1]
    merged = jnp.concatenate([w_values, w_states, w_gates, w_steps], axis=1)
    full = lax.all_gather(merged, "seq", axis=0, tiled=True)
    projected = jnp.dot(block_hidden, full, preferred_element_type=jnp.float32)
    conv_end = local_width + 2 * state_width
    pre_rows = projected[:, :conv_end].astype(jnp.bfloat16)
    gates_sum = projected[:, conv_end : conv_end + local_width]
    steps_sum = projected[:, conv_end + local_width : conv_end + local_width + step_width]
    local_taps = jnp.concatenate(
        [
            lax.dynamic_slice_in_dim(conv_weight, group_index * local_width, local_width, 1),
            conv_weight[:, inner_width:],
        ],
        axis=1,
    )
    local_bias = jnp.concatenate(
        [
            lax.dynamic_slice_in_dim(conv_bias, group_index * local_width, local_width, 0),
            conv_bias[inner_width:],
        ],
        axis=0,
    )
    block_start = block_index * block_rows
    rim_rows = pre_rows[block_rows - (conv_taps - 1) :]
    prior_rim = from_behind(rim_rows, "seq", 1)
    extended = jnp.concatenate([prior_rim, pre_rows], axis=0)
    ext_positions = (
        block_start - (conv_taps - 1) + jnp.arange(block_rows + conv_taps - 1, dtype=jnp.int32)
    )
    ext_ids = segments_at(ext_positions, prompt_ends)
    own_ids = ext_ids[conv_taps - 1 :]
    filtered = jnp.zeros(pre_rows.shape, jnp.float32) + local_bias[None, :]
    for offset in range(conv_taps):
        matches = (ext_ids[offset : offset + block_rows] == own_ids).astype(jnp.float32)
        filtered = (
            filtered
            + local_taps[offset][None, :]
            * extended[offset : offset + block_rows].astype(jnp.float32)
            * matches[:, None]
        )
    conv_out = jax.nn.silu(filtered).astype(jnp.bfloat16)
    head_values = conv_out[:, :local_width]
    both_states = conv_out[:, local_width:]
    stretch_rows = STRETCH
    stretches = block_rows // stretch_rows
    positions = block_start + jnp.arange(block_rows, dtype=jnp.int32)
    segment_ids = segments_at(positions, prompt_ends)
    next_ids = segments_at(positions + 1, prompt_ends)
    before_ids = segments_at(positions - 1, prompt_ends)
    stretch_ids = segment_ids.reshape(stretches, stretch_rows)
    prior_ids = before_ids.reshape(stretches, stretch_rows)[:, 0]
    ends_mask = (segment_ids != next_ids).reshape(stretches, stretch_rows)
    step_sizes = jax.nn.softplus(steps_sum + step_bias[None, :])
    decay_steps = step_sizes * decay_rate[None, :]
    log_decay = -jnp.cumsum(decay_steps.reshape(stretches, stretch_rows, local_heads), axis=1)
    decay_heads = jnp.swapaxes(log_decay, 1, 2)
    step_heads = jnp.swapaxes(step_sizes.reshape(stretches, stretch_rows, local_heads), 1, 2)
    values = head_values.reshape(stretches, stretch_rows, local_heads, head_width)
    write_state = both_states[:, :state_width].reshape(stretches, stretch_rows, state_width)
    read_state = both_states[:, state_width:].reshape(stretches, stretch_rows, state_width)
    intersection = jnp.einsum(
        "ctn,csn->cts", read_state, write_state, preferred_element_type=jnp.float32
    )
    token_order = jnp.arange(stretch_rows, dtype=jnp.int32)
    causal = token_order[:, None] >= token_order[None, :]
    allowed = causal[None] & (stretch_ids[:, :, None] == stretch_ids[:, None, :])
    spread = decay_heads[:, :, :, None] - decay_heads[:, :, None, :]
    weights = (
        jnp.where(allowed[:, None], jnp.exp(jnp.minimum(spread, 0.0)), 0.0)
        * step_heads[:, :, None, :]
    )
    scores = (intersection[:, None] * weights).astype(jnp.bfloat16)
    within_stretch = jnp.einsum(
        "chts,cshp->cthp", scores, values, preferred_element_type=jnp.float32
    )
    last_ids = stretch_ids[:, -1]
    tail_decay = decay_heads[:, :, -1:]
    keep_tail = (stretch_ids == last_ids[:, None])[:, None, :]
    tail_coef = (
        jnp.where(keep_tail, jnp.exp(jnp.minimum(tail_decay - decay_heads, 0.0)), 0.0) * step_heads
    )
    tail_rows = (values.astype(jnp.float32) * jnp.swapaxes(tail_coef, 1, 2)[:, :, :, None]).astype(
        jnp.bfloat16
    )
    stretch_states = jnp.einsum(
        "clhp,cln->chpn", tail_rows, write_state, preferred_element_type=jnp.float32
    )
    stretch_gates = (
        jnp.exp(decay_heads[:, :, -1]) * (last_ids == prior_ids).astype(jnp.float32)[:, None]
    )
    own_pair = (stretch_gates[0], stretch_states[0])
    g1, s1 = from_behind(own_pair, "seq", 1)
    g2, s2 = from_behind(own_pair, "seq", 2)
    g3, s3 = from_behind(own_pair, "seq", 3)
    incoming = s1 + g1[:, None, None] * (s2 + g2[:, None, None] * s3)
    arriving = incoming[None]
    carry_mask = (stretch_ids == prior_ids[:, None]).astype(jnp.float32)
    carry_decay = jnp.exp(log_decay) * carry_mask[:, :, None]
    from_before = (
        jnp.einsum(
            "cln,chpn->clhp",
            read_state,
            arriving.astype(jnp.bfloat16),
            preferred_element_type=jnp.float32,
        )
        * carry_decay[:, :, :, None]
    )
    result = (
        within_stretch + from_before + skip_gain[None, None, :, None] * values.astype(jnp.float32)
    )
    ssm_rows = result.reshape(block_rows, local_width).astype(jnp.bfloat16)
    end_weight = ends_mask.astype(jnp.float32)
    has_end = jnp.sum(end_weight, axis=1)
    end_decay = jnp.sum(decay_heads * end_weight[:, None, :], axis=2)
    end_ids = jnp.sum(jnp.where(ends_mask, stretch_ids, 0), axis=1)
    keep_end = ((stretch_ids == end_ids[:, None]) & (has_end[:, None] > 0))[:, None, :]
    end_coef = (
        jnp.where(keep_end, jnp.exp(jnp.minimum(end_decay[:, :, None] - decay_heads, 0.0)), 0.0)
        * step_heads
    )
    end_rows = (values.astype(jnp.float32) * jnp.swapaxes(end_coef, 1, 2)[:, :, :, None]).astype(
        jnp.bfloat16
    )
    end_states = jnp.einsum(
        "clhp,cln->chpn", end_rows, write_state, preferred_element_type=jnp.float32
    )
    end_carry = (
        jnp.exp(end_decay) * ((end_ids == prior_ids) & (has_end > 0)).astype(jnp.float32)[:, None]
    )
    end_states = end_states + end_carry[:, :, None, None] * arriving
    final_block = jnp.sum(end_states, axis=0)[None]
    head_gates = gates_sum.astype(jnp.bfloat16)
    both = jnp.stack([ssm_rows, head_gates]).reshape(2, groups, sub_rows, local_width)
    returned = lax.all_to_all(both, "head", split_axis=1, concat_axis=3, tiled=True)
    token_rows = returned.reshape(2, sub_rows, inner_width).astype(jnp.float32)
    gated = token_rows[0] * jax.nn.silu(token_rows[1])
    mean_square = jnp.mean(gated * gated, axis=1)
    scaled = gated * lax.rsqrt(mean_square + epsilon)[:, None] * norm_gain[None, :]
    gated_out = scaled.astype(jnp.bfloat16)
    return (gated_out, final_block)


def solution(mesh):
    in_specs = (
        P(("seq", "head"), None),
        P("seq", "head"),
        P("seq", "head"),
        P("seq", "head"),
        P("seq", None),
        P(),
        P(),
        P("head"),
        P("head"),
        P("head"),
        P(),
        P(),
    )
    out_specs = (P(("seq", "head"), None), P("seq", "head", None, None))
    return jax.shard_map(
        on_device, mesh=mesh, in_specs=in_specs, out_specs=out_specs, check_vma=False
    )
```

```python
import jax
import jax.numpy as jnp
from jax import lax
from jax.sharding import PartitionSpec as P

STRETCH = 256


epsilon = 1e-05


def from_behind(block, axis, distance):
    devices = range(lax.axis_size(axis))
    route = [(i - distance, i) for i in devices if i - distance in devices]
    return lax.ppermute(block, axis, route)


def segments_at(positions, prompt_ends):
    counted = jnp.sum((prompt_ends[None, :] <= positions[:, None]).astype(jnp.int32), axis=1)
    return jnp.where(positions < 0, -1, counted)


def on_device(
    hidden,
    w_values,
    w_gates,
    w_steps,
    w_states,
    conv_weight,
    conv_bias,
    step_bias,
    decay_rate,
    skip_gain,
    norm_gain,
    lengths,
):
    groups = lax.axis_size("head")
    group_index = lax.axis_index("head")
    block_index = lax.axis_index("seq")
    local_width = w_values.shape[1]
    inner_width = local_width * groups
    local_heads = decay_rate.shape[0]
    head_width = local_width // local_heads
    state_width = w_states.shape[1] // 2
    conv_taps = conv_weight.shape[0]
    prompt_ends = jnp.cumsum(lengths)
    block_hidden = lax.all_to_all(
        jnp.broadcast_to(hidden[None], (groups,) + hidden.shape), "head", 0, 0, tiled=True
    ).reshape(groups * hidden.shape[0], hidden.shape[1])
    block_rows = block_hidden.shape[0]
    sub_rows = block_rows // groups
    step_width = w_steps.shape[1]
    merged = jnp.concatenate([w_values, w_states, w_gates, w_steps], axis=1)
    shard_rows = merged.shape[0]
    padded_rows = -(-shard_rows // 16) * 16
    merged = jnp.pad(merged, ((0, padded_rows - shard_rows), (0, 0)))
    full = lax.all_gather(merged, "seq", axis=0, tiled=True)
    shards = full.shape[0] // padded_rows

    def spread_rows(rows):
        count = rows.shape[0]
        split = rows.reshape(count, shards, shard_rows)
        split = jnp.pad(split, ((0, 0), (0, 0), (0, padded_rows - shard_rows)))
        return split.reshape(count, shards * padded_rows)

    rim_hidden = from_behind(block_hidden[block_rows - (conv_taps - 1) :], "seq", 1)
    projected = jnp.dot(spread_rows(block_hidden), full, preferred_element_type=jnp.float32)
    rim_projected = jnp.dot(spread_rows(rim_hidden), full, preferred_element_type=jnp.float32)
    conv_end = local_width + 2 * state_width
    pre_rows = projected[:, :conv_end].astype(jnp.bfloat16)
    prior_rim = rim_projected[:, :conv_end].astype(jnp.bfloat16)
    gates_sum = projected[:, conv_end : conv_end + local_width]
    steps_sum = projected[:, conv_end + local_width : conv_end + local_width + step_width]
    head_gates = gates_sum.astype(jnp.bfloat16)
    gates_tokens = lax.all_to_all(
        head_gates.reshape(groups, sub_rows, local_width), "head", 0, 2, tiled=True
    ).reshape(sub_rows, inner_width)
    local_taps = jnp.concatenate(
        [
            lax.dynamic_slice_in_dim(conv_weight, group_index * local_width, local_width, 1),
            conv_weight[:, inner_width:],
        ],
        axis=1,
    )
    local_bias = jnp.concatenate(
        [
            lax.dynamic_slice_in_dim(conv_bias, group_index * local_width, local_width, 0),
            conv_bias[inner_width:],
        ],
        axis=0,
    )
    block_start = block_index * block_rows
    extended = jnp.concatenate([prior_rim, pre_rows], axis=0)
    ext_positions = (
        block_start - (conv_taps - 1) + jnp.arange(block_rows + conv_taps - 1, dtype=jnp.int32)
    )
    ext_ids = segments_at(ext_positions, prompt_ends)
    own_ids = ext_ids[conv_taps - 1 :]
    filtered = jnp.zeros(pre_rows.shape, jnp.float32) + local_bias[None, :]
    for offset in range(conv_taps):
        matches = (ext_ids[offset : offset + block_rows] == own_ids).astype(jnp.float32)
        filtered = (
            filtered
            + local_taps[offset][None, :]
            * extended[offset : offset + block_rows].astype(jnp.float32)
            * matches[:, None]
        )
    conv_out = jax.nn.silu(filtered).astype(jnp.bfloat16)
    head_values = conv_out[:, :local_width]
    both_states = conv_out[:, local_width:]
    stretch_rows = STRETCH
    stretches = block_rows // stretch_rows
    positions = block_start + jnp.arange(block_rows, dtype=jnp.int32)
    segment_ids = segments_at(positions, prompt_ends)
    next_ids = segments_at(positions + 1, prompt_ends)
    before_ids = segments_at(positions - 1, prompt_ends)
    stretch_ids = segment_ids.reshape(stretches, stretch_rows)
    prior_ids = before_ids.reshape(stretches, stretch_rows)[:, 0]
    ends_mask = (segment_ids != next_ids).reshape(stretches, stretch_rows)
    step_sizes = jax.nn.softplus(steps_sum + step_bias[None, :])
    decay_steps = step_sizes * decay_rate[None, :]
    log_decay = -jnp.cumsum(decay_steps.reshape(stretches, stretch_rows, local_heads), axis=1)
    decay_heads = jnp.swapaxes(log_decay, 1, 2)
    step_heads = jnp.swapaxes(step_sizes.reshape(stretches, stretch_rows, local_heads), 1, 2)
    values = head_values.reshape(stretches, stretch_rows, local_heads, head_width)
    write_state = both_states[:, :state_width].reshape(stretches, stretch_rows, state_width)
    read_state = both_states[:, state_width:].reshape(stretches, stretch_rows, state_width)
    intersection = jnp.einsum(
        "ctn,csn->cts", read_state, write_state, preferred_element_type=jnp.float32
    )
    token_order = jnp.arange(stretch_rows, dtype=jnp.int32)
    causal = token_order[:, None] >= token_order[None, :]
    allowed = causal[None] & (stretch_ids[:, :, None] == stretch_ids[:, None, :])
    spread = decay_heads[:, :, :, None] - decay_heads[:, :, None, :]
    weights = (
        jnp.where(allowed[:, None], jnp.exp(jnp.minimum(spread, 0.0)), 0.0)
        * step_heads[:, :, None, :]
    )
    scores = (intersection[:, None] * weights).astype(jnp.bfloat16)
    within_stretch = jnp.einsum(
        "chts,cshp->cthp", scores, values, preferred_element_type=jnp.float32
    )
    last_ids = stretch_ids[:, -1]
    tail_decay = decay_heads[:, :, -1:]
    keep_tail = (stretch_ids == last_ids[:, None])[:, None, :]
    tail_coef = (
        jnp.where(keep_tail, jnp.exp(jnp.minimum(tail_decay - decay_heads, 0.0)), 0.0) * step_heads
    )
    tail_rows = (values.astype(jnp.float32) * jnp.swapaxes(tail_coef, 1, 2)[:, :, :, None]).astype(
        jnp.bfloat16
    )
    stretch_states = jnp.einsum(
        "clhp,cln->chpn", tail_rows, write_state, preferred_element_type=jnp.float32
    )
    stretch_gates = (
        jnp.exp(decay_heads[:, :, -1]) * (last_ids == prior_ids).astype(jnp.float32)[:, None]
    )
    own_gate = jnp.broadcast_to(stretch_gates[0][:, None, None], (local_heads, 8, state_width))
    packed = jnp.concatenate([stretch_states[0], own_gate], axis=1)
    p1 = from_behind(packed, "seq", 1)
    p2 = from_behind(packed, "seq", 2)
    p3 = from_behind(packed, "seq", 3)
    g1 = p1[:, head_width : head_width + 1, :1]
    g2 = p2[:, head_width : head_width + 1, :1]
    incoming = p1[:, :head_width] + g1 * (p2[:, :head_width] + g2 * p3[:, :head_width])
    arriving = incoming[None]
    carry_mask = (stretch_ids == prior_ids[:, None]).astype(jnp.float32)
    carry_decay = jnp.exp(log_decay) * carry_mask[:, :, None]
    from_before = (
        jnp.einsum(
            "cln,chpn->clhp",
            read_state,
            arriving.astype(jnp.bfloat16),
            preferred_element_type=jnp.float32,
        )
        * carry_decay[:, :, :, None]
    )
    result = (
        within_stretch + from_before + skip_gain[None, None, :, None] * values.astype(jnp.float32)
    )
    ssm_rows = result.reshape(block_rows, local_width).astype(jnp.bfloat16)
    end_weight = ends_mask.astype(jnp.float32)
    has_end = jnp.sum(end_weight, axis=1)
    end_decay = jnp.sum(decay_heads * end_weight[:, None, :], axis=2)
    end_ids = jnp.sum(jnp.where(ends_mask, stretch_ids, 0), axis=1)
    keep_end = ((stretch_ids == end_ids[:, None]) & (has_end[:, None] > 0))[:, None, :]
    end_coef = (
        jnp.where(keep_end, jnp.exp(jnp.minimum(end_decay[:, :, None] - decay_heads, 0.0)), 0.0)
        * step_heads
    )
    end_rows = (values.astype(jnp.float32) * jnp.swapaxes(end_coef, 1, 2)[:, :, :, None]).astype(
        jnp.bfloat16
    )
    end_states = jnp.einsum(
        "clhp,cln->chpn", end_rows, write_state, preferred_element_type=jnp.float32
    )
    end_carry = (
        jnp.exp(end_decay) * ((end_ids == prior_ids) & (has_end > 0)).astype(jnp.float32)[:, None]
    )
    end_states = end_states + end_carry[:, :, None, None] * arriving
    final_block = jnp.sum(end_states, axis=0)[None]
    y_tokens = lax.all_to_all(
        ssm_rows.reshape(groups, sub_rows, local_width), "head", 0, 2, tiled=True
    ).reshape(sub_rows, inner_width)
    token_rows = (y_tokens.astype(jnp.float32), gates_tokens.astype(jnp.float32))
    gated = token_rows[0] * jax.nn.silu(token_rows[1])
    mean_square = jnp.mean(gated * gated, axis=1)
    scaled = gated * lax.rsqrt(mean_square + epsilon)[:, None] * norm_gain[None, :]
    gated_out = scaled.astype(jnp.bfloat16)
    return (gated_out, final_block)


def solution(mesh):
    in_specs = (
        P(("seq", "head"), None),
        P("seq", "head"),
        P("seq", "head"),
        P("seq", "head"),
        P("seq", None),
        P(),
        P(),
        P("head"),
        P("head"),
        P("head"),
        P(),
        P(),
    )
    out_specs = (P(("seq", "head"), None), P("seq", "head", None, None))
    return jax.shard_map(
        on_device, mesh=mesh, in_specs=in_specs, out_specs=out_specs, check_vma=False
    )
```

```python
import jax
import jax.numpy as jnp
from jax import lax
from jax.sharding import PartitionSpec as P

STRETCH = 256


epsilon = 1e-05


def from_behind(block, axis, distance):
    devices = range(lax.axis_size(axis))
    route = [(i - distance, i) for i in devices if i - distance in devices]
    return lax.ppermute(block, axis, route)


def segments_at(positions, prompt_ends):
    counted = jnp.sum((prompt_ends[None, :] <= positions[:, None]).astype(jnp.int32), axis=1)
    return jnp.where(positions < 0, -1, counted)


def on_device(
    hidden,
    w_values,
    w_gates,
    w_steps,
    w_states,
    conv_weight,
    conv_bias,
    step_bias,
    decay_rate,
    skip_gain,
    norm_gain,
    lengths,
):
    groups = lax.axis_size("head")
    group_index = lax.axis_index("head")
    block_index = lax.axis_index("seq")
    local_width = w_values.shape[1]
    inner_width = local_width * groups
    local_heads = decay_rate.shape[0]
    head_width = local_width // local_heads
    state_width = w_states.shape[1] // 2
    conv_taps = conv_weight.shape[0]
    prompt_ends = jnp.cumsum(lengths)
    block_hidden = lax.all_to_all(
        jnp.broadcast_to(hidden[None], (groups,) + hidden.shape), "head", 0, 0, tiled=True
    ).reshape(groups * hidden.shape[0], hidden.shape[1])
    block_rows = block_hidden.shape[0]
    sub_rows = block_rows // groups
    step_width = w_steps.shape[1]
    merged = jnp.concatenate([w_values, w_states, w_gates, w_steps], axis=1)
    shard_rows = merged.shape[0]
    padded_rows = -(-shard_rows // 16) * 16
    merged = jnp.pad(merged, ((0, padded_rows - shard_rows), (0, 0)))
    full = lax.all_gather(merged, "seq", axis=0, tiled=True)
    shards = full.shape[0] // padded_rows

    def spread_rows(rows):
        count = rows.shape[0]
        split = rows.reshape(count, shards, shard_rows)
        split = jnp.pad(split, ((0, 0), (0, 0), (0, padded_rows - shard_rows)))
        return split.reshape(count, shards * padded_rows)

    rim_hidden = from_behind(block_hidden[block_rows - (conv_taps - 1) :], "seq", 1)
    rim_count = rim_hidden.shape[0]
    both_rows = jnp.concatenate(
        [block_hidden, rim_hidden, jnp.zeros((8 - rim_count, block_hidden.shape[1]), jnp.bfloat16)]
    )
    projected = jnp.dot(spread_rows(both_rows), full, preferred_element_type=jnp.float32)
    conv_end = local_width + 2 * state_width
    prior_rim = projected[block_rows : block_rows + rim_count, :conv_end].astype(jnp.bfloat16)
    projected = projected[:block_rows]
    pre_rows = projected[:, :conv_end].astype(jnp.bfloat16)
    gates_sum = projected[:, conv_end : conv_end + local_width]
    steps_sum = projected[:, conv_end + local_width : conv_end + local_width + step_width]
    head_gates = gates_sum.astype(jnp.bfloat16)
    gates_tokens = lax.all_to_all(
        head_gates.reshape(groups, sub_rows, local_width), "head", 0, 2, tiled=True
    ).reshape(sub_rows, inner_width)
    local_taps = jnp.concatenate(
        [
            lax.dynamic_slice_in_dim(conv_weight, group_index * local_width, local_width, 1),
            conv_weight[:, inner_width:],
        ],
        axis=1,
    )
    local_bias = jnp.concatenate(
        [
            lax.dynamic_slice_in_dim(conv_bias, group_index * local_width, local_width, 0),
            conv_bias[inner_width:],
        ],
        axis=0,
    )
    block_start = block_index * block_rows
    extended = jnp.concatenate([prior_rim, pre_rows], axis=0)
    ext_positions = (
        block_start - (conv_taps - 1) + jnp.arange(block_rows + conv_taps - 1, dtype=jnp.int32)
    )
    ext_ids = segments_at(ext_positions, prompt_ends)
    own_ids = ext_ids[conv_taps - 1 :]
    filtered = jnp.zeros(pre_rows.shape, jnp.float32) + local_bias[None, :]
    for offset in range(conv_taps):
        matches = (ext_ids[offset : offset + block_rows] == own_ids).astype(jnp.float32)
        filtered = (
            filtered
            + local_taps[offset][None, :]
            * extended[offset : offset + block_rows].astype(jnp.float32)
            * matches[:, None]
        )
    conv_out = jax.nn.silu(filtered).astype(jnp.bfloat16)
    head_values = conv_out[:, :local_width]
    both_states = conv_out[:, local_width:]
    stretch_rows = STRETCH
    stretches = block_rows // stretch_rows
    positions = block_start + jnp.arange(block_rows, dtype=jnp.int32)
    segment_ids = segments_at(positions, prompt_ends)
    next_ids = segments_at(positions + 1, prompt_ends)
    before_ids = segments_at(positions - 1, prompt_ends)
    stretch_ids = segment_ids.reshape(stretches, stretch_rows)
    prior_ids = before_ids.reshape(stretches, stretch_rows)[:, 0]
    ends_mask = (segment_ids != next_ids).reshape(stretches, stretch_rows)
    step_sizes = jax.nn.softplus(steps_sum + step_bias[None, :])
    decay_steps = step_sizes * decay_rate[None, :]
    log_decay = -jnp.cumsum(decay_steps.reshape(stretches, stretch_rows, local_heads), axis=1)
    decay_heads = jnp.swapaxes(log_decay, 1, 2)
    step_heads = jnp.swapaxes(step_sizes.reshape(stretches, stretch_rows, local_heads), 1, 2)
    values = head_values.reshape(stretches, stretch_rows, local_heads, head_width)
    write_state = both_states[:, :state_width].reshape(stretches, stretch_rows, state_width)
    read_state = both_states[:, state_width:].reshape(stretches, stretch_rows, state_width)
    intersection = jnp.einsum(
        "ctn,csn->cts", read_state, write_state, preferred_element_type=jnp.float32
    )
    token_order = jnp.arange(stretch_rows, dtype=jnp.int32)
    causal = token_order[:, None] >= token_order[None, :]
    allowed = causal[None] & (stretch_ids[:, :, None] == stretch_ids[:, None, :])
    spread = decay_heads[:, :, :, None] - decay_heads[:, :, None, :]
    weights = (
        jnp.where(allowed[:, None], jnp.exp(jnp.minimum(spread, 0.0)), 0.0)
        * step_heads[:, :, None, :]
    )
    scores = (intersection[:, None] * weights).astype(jnp.bfloat16)
    within_stretch = jnp.einsum(
        "chts,cshp->cthp", scores, values, preferred_element_type=jnp.float32
    )
    last_ids = stretch_ids[:, -1]
    tail_decay = decay_heads[:, :, -1:]
    keep_tail = (stretch_ids == last_ids[:, None])[:, None, :]
    tail_coef = (
        jnp.where(keep_tail, jnp.exp(jnp.minimum(tail_decay - decay_heads, 0.0)), 0.0) * step_heads
    )
    tail_rows = (values.astype(jnp.float32) * jnp.swapaxes(tail_coef, 1, 2)[:, :, :, None]).astype(
        jnp.bfloat16
    )
    stretch_states = jnp.einsum(
        "clhp,cln->chpn", tail_rows, write_state, preferred_element_type=jnp.float32
    )
    stretch_gates = (
        jnp.exp(decay_heads[:, :, -1]) * (last_ids == prior_ids).astype(jnp.float32)[:, None]
    )
    own_gate = jnp.broadcast_to(stretch_gates[0][:, None, None], (local_heads, 8, state_width))
    packed = jnp.concatenate([stretch_states[0], own_gate], axis=1).astype(jnp.bfloat16)
    p1 = from_behind(packed, "seq", 1)
    p2 = from_behind(packed, "seq", 2)
    p3 = from_behind(packed, "seq", 3)
    g1 = p1[:, head_width : head_width + 1, :1]
    g2 = p2[:, head_width : head_width + 1, :1]
    p1, p2, p3, g1, g2 = (part.astype(jnp.float32) for part in (p1, p2, p3, g1, g2))
    incoming = p1[:, :head_width] + g1 * (p2[:, :head_width] + g2 * p3[:, :head_width])
    arriving = incoming[None]
    carry_mask = (stretch_ids == prior_ids[:, None]).astype(jnp.float32)
    carry_decay = jnp.exp(log_decay) * carry_mask[:, :, None]
    from_before = (
        jnp.einsum(
            "cln,chpn->clhp",
            read_state,
            arriving.astype(jnp.bfloat16),
            preferred_element_type=jnp.float32,
        )
        * carry_decay[:, :, :, None]
    )
    result = (
        within_stretch + from_before + skip_gain[None, None, :, None] * values.astype(jnp.float32)
    )
    ssm_rows = result.reshape(block_rows, local_width).astype(jnp.bfloat16)
    end_weight = ends_mask.astype(jnp.float32)
    has_end = jnp.sum(end_weight, axis=1)
    end_decay = jnp.sum(decay_heads * end_weight[:, None, :], axis=2)
    end_ids = jnp.sum(jnp.where(ends_mask, stretch_ids, 0), axis=1)
    keep_end = ((stretch_ids == end_ids[:, None]) & (has_end[:, None] > 0))[:, None, :]
    end_coef = (
        jnp.where(keep_end, jnp.exp(jnp.minimum(end_decay[:, :, None] - decay_heads, 0.0)), 0.0)
        * step_heads
    )
    end_rows = (values.astype(jnp.float32) * jnp.swapaxes(end_coef, 1, 2)[:, :, :, None]).astype(
        jnp.bfloat16
    )
    end_states = jnp.einsum(
        "clhp,cln->chpn", end_rows, write_state, preferred_element_type=jnp.float32
    )
    end_carry = (
        jnp.exp(end_decay) * ((end_ids == prior_ids) & (has_end > 0)).astype(jnp.float32)[:, None]
    )
    end_states = end_states + end_carry[:, :, None, None] * arriving
    final_block = jnp.sum(end_states, axis=0)[None]
    y_tokens = lax.all_to_all(
        ssm_rows.reshape(groups, sub_rows, local_width), "head", 0, 2, tiled=True
    ).reshape(sub_rows, inner_width)
    token_rows = (y_tokens.astype(jnp.float32), gates_tokens.astype(jnp.float32))
    gated = token_rows[0] * jax.nn.silu(token_rows[1])
    mean_square = jnp.mean(gated * gated, axis=1)
    scaled = gated * lax.rsqrt(mean_square + epsilon)[:, None] * norm_gain[None, :]
    gated_out = scaled.astype(jnp.bfloat16)
    return (gated_out, final_block)


def solution(mesh):
    in_specs = (
        P(("seq", "head"), None),
        P("seq", "head"),
        P("seq", "head"),
        P("seq", "head"),
        P("seq", None),
        P(),
        P(),
        P("head"),
        P("head"),
        P("head"),
        P(),
        P(),
    )
    out_specs = (P(("seq", "head"), None), P("seq", "head", None, None))
    return jax.shard_map(
        on_device, mesh=mesh, in_specs=in_specs, out_specs=out_specs, check_vma=False
    )
```

```python
import jax
import jax.numpy as jnp
from jax import lax
from jax.sharding import Mesh, PartitionSpec as P

STRETCH = 256
SEQ = ("x", "z", "c")


epsilon = 1e-05


def from_behind(block, axis, distance):
    devices = range(lax.psum(1, axis))
    route = [(i - distance, i) for i in devices if i - distance in devices]
    return lax.ppermute(block, axis, route)


def segments_at(positions, prompt_ends):
    counted = jnp.sum((prompt_ends[None, :] <= positions[:, None]).astype(jnp.int32), axis=1)
    return jnp.where(positions < 0, -1, counted)


def on_device(
    hidden,
    w_values,
    w_gates,
    w_steps,
    w_states,
    conv_weight,
    conv_bias,
    step_bias,
    decay_rate,
    skip_gain,
    norm_gain,
    lengths,
):
    groups = lax.axis_size("head")
    group_index = lax.axis_index("head")
    block_index = lax.axis_index(SEQ)
    local_width = w_values.shape[1]
    inner_width = local_width * groups
    local_heads = decay_rate.shape[0]
    head_width = local_width // local_heads
    state_width = w_states.shape[1] // 2
    conv_taps = conv_weight.shape[0]
    prompt_ends = jnp.cumsum(lengths)
    block_hidden = lax.all_to_all(
        jnp.broadcast_to(hidden[None], (groups,) + hidden.shape), "head", 0, 0, tiled=True
    ).reshape(groups * hidden.shape[0], hidden.shape[1])
    block_rows = block_hidden.shape[0]
    sub_rows = block_rows // groups
    step_width = w_steps.shape[1]
    merged = jnp.concatenate([w_values, w_states, w_gates, w_steps], axis=1)
    shard_rows = merged.shape[0]
    padded_rows = -(-shard_rows // 16) * 16
    half = local_width + 2 * state_width
    merged = jnp.pad(merged, ((0, padded_rows - shard_rows), (0, 2 * half - merged.shape[1])))
    halves = jnp.stack([merged[:, :half], merged[:, half:]])
    own_half = lax.all_to_all(halves, "c", 0, 0, tiled=True).reshape(2 * padded_rows, half)
    own_half = lax.all_gather(own_half, "x", axis=0, tiled=True)
    own_half = lax.all_gather(own_half, "z", axis=0, tiled=True)
    other_half = lax.ppermute(own_half, "c", [(0, 1), (1, 0)])
    x_size = lax.psum(1, "x")
    z_size = lax.psum(1, "z")
    c_size = lax.psum(1, "c")
    core_index = lax.axis_index("c")

    def spread_rows(rows):
        count = rows.shape[0]
        split = rows.reshape(count, x_size, z_size, c_size, shard_rows)
        split = jnp.pad(split, ((0, 0), (0, 0), (0, 0), (0, 0), (0, padded_rows - shard_rows)))
        split = jnp.transpose(split, (0, 2, 1, 3, 4))
        return split.reshape(count, x_size * z_size * c_size * padded_rows)

    rim_hidden = from_behind(block_hidden[block_rows - (conv_taps - 1) :], SEQ, 1)
    rim_count = rim_hidden.shape[0]
    both_rows = jnp.concatenate(
        [block_hidden, rim_hidden, jnp.zeros((8 - rim_count, block_hidden.shape[1]), jnp.bfloat16)]
    )
    spread = spread_rows(both_rows)
    with_own = jnp.dot(spread, own_half, preferred_element_type=jnp.float32)
    with_other = jnp.dot(spread, other_half, preferred_element_type=jnp.float32)
    first_cols = jnp.where(core_index == 0, with_own, with_other)
    second_cols = jnp.where(core_index == 0, with_other, with_own)
    projected = jnp.concatenate([first_cols, second_cols], axis=1)
    conv_end = local_width + 2 * state_width
    prior_rim = projected[block_rows : block_rows + rim_count, :conv_end].astype(jnp.bfloat16)
    projected = projected[:block_rows]
    pre_rows = projected[:, :conv_end].astype(jnp.bfloat16)
    gates_sum = projected[:, conv_end : conv_end + local_width]
    steps_sum = projected[:, conv_end + local_width : conv_end + local_width + step_width]
    head_gates = gates_sum.astype(jnp.bfloat16)
    gates_tokens = lax.all_to_all(
        head_gates.reshape(groups, sub_rows, local_width), "head", 0, 2, tiled=True
    ).reshape(sub_rows, inner_width)
    local_taps = jnp.concatenate(
        [
            lax.dynamic_slice_in_dim(conv_weight, group_index * local_width, local_width, 1),
            conv_weight[:, inner_width:],
        ],
        axis=1,
    )
    local_bias = jnp.concatenate(
        [
            lax.dynamic_slice_in_dim(conv_bias, group_index * local_width, local_width, 0),
            conv_bias[inner_width:],
        ],
        axis=0,
    )
    block_start = block_index * block_rows
    extended = jnp.concatenate([prior_rim, pre_rows], axis=0)
    ext_positions = (
        block_start - (conv_taps - 1) + jnp.arange(block_rows + conv_taps - 1, dtype=jnp.int32)
    )
    ext_ids = segments_at(ext_positions, prompt_ends)
    own_ids = ext_ids[conv_taps - 1 :]
    filtered = jnp.zeros(pre_rows.shape, jnp.float32) + local_bias[None, :]
    for offset in range(conv_taps):
        matches = (ext_ids[offset : offset + block_rows] == own_ids).astype(jnp.float32)
        filtered = (
            filtered
            + local_taps[offset][None, :]
            * extended[offset : offset + block_rows].astype(jnp.float32)
            * matches[:, None]
        )
    conv_out = jax.nn.silu(filtered).astype(jnp.bfloat16)
    head_values = conv_out[:, :local_width]
    both_states = conv_out[:, local_width:]
    stretch_rows = STRETCH
    stretches = block_rows // stretch_rows
    positions = block_start + jnp.arange(block_rows, dtype=jnp.int32)
    segment_ids = segments_at(positions, prompt_ends)
    next_ids = segments_at(positions + 1, prompt_ends)
    before_ids = segments_at(positions - 1, prompt_ends)
    stretch_ids = segment_ids.reshape(stretches, stretch_rows)
    prior_ids = before_ids.reshape(stretches, stretch_rows)[:, 0]
    ends_mask = (segment_ids != next_ids).reshape(stretches, stretch_rows)
    step_sizes = jax.nn.softplus(steps_sum + step_bias[None, :])
    decay_steps = step_sizes * decay_rate[None, :]
    log_decay = -jnp.cumsum(decay_steps.reshape(stretches, stretch_rows, local_heads), axis=1)
    decay_heads = jnp.swapaxes(log_decay, 1, 2)
    step_heads = jnp.swapaxes(step_sizes.reshape(stretches, stretch_rows, local_heads), 1, 2)
    values = head_values.reshape(stretches, stretch_rows, local_heads, head_width)
    write_state = both_states[:, :state_width].reshape(stretches, stretch_rows, state_width)
    read_state = both_states[:, state_width:].reshape(stretches, stretch_rows, state_width)
    intersection = jnp.einsum(
        "ctn,csn->cts", read_state, write_state, preferred_element_type=jnp.float32
    )
    token_order = jnp.arange(stretch_rows, dtype=jnp.int32)
    causal = token_order[:, None] >= token_order[None, :]
    allowed = causal[None] & (stretch_ids[:, :, None] == stretch_ids[:, None, :])
    spread = decay_heads[:, :, :, None] - decay_heads[:, :, None, :]
    weights = (
        jnp.where(allowed[:, None], jnp.exp(jnp.minimum(spread, 0.0)), 0.0)
        * step_heads[:, :, None, :]
    )
    scores = (intersection[:, None] * weights).astype(jnp.bfloat16)
    within_stretch = jnp.einsum(
        "chts,cshp->cthp", scores, values, preferred_element_type=jnp.float32
    )
    last_ids = stretch_ids[:, -1]
    tail_decay = decay_heads[:, :, -1:]
    keep_tail = (stretch_ids == last_ids[:, None])[:, None, :]
    tail_coef = (
        jnp.where(keep_tail, jnp.exp(jnp.minimum(tail_decay - decay_heads, 0.0)), 0.0) * step_heads
    )
    tail_rows = (values.astype(jnp.float32) * jnp.swapaxes(tail_coef, 1, 2)[:, :, :, None]).astype(
        jnp.bfloat16
    )
    stretch_states = jnp.einsum(
        "clhp,cln->chpn", tail_rows, write_state, preferred_element_type=jnp.float32
    )
    stretch_gates = (
        jnp.exp(decay_heads[:, :, -1]) * (last_ids == prior_ids).astype(jnp.float32)[:, None]
    )
    own_gate = jnp.broadcast_to(stretch_gates[0][:, None, None], (local_heads, 8, state_width))
    packed = jnp.concatenate([stretch_states[0], own_gate], axis=1).astype(jnp.bfloat16)
    p1 = from_behind(packed, SEQ, 1)
    p2 = from_behind(packed, SEQ, 2)
    p3 = from_behind(packed, SEQ, 3)
    g1 = p1[:, head_width : head_width + 1, :1]
    g2 = p2[:, head_width : head_width + 1, :1]
    p1, p2, p3, g1, g2 = (part.astype(jnp.float32) for part in (p1, p2, p3, g1, g2))
    incoming = p1[:, :head_width] + g1 * (p2[:, :head_width] + g2 * p3[:, :head_width])
    arriving = incoming[None]
    carry_mask = (stretch_ids == prior_ids[:, None]).astype(jnp.float32)
    carry_decay = jnp.exp(log_decay) * carry_mask[:, :, None]
    from_before = (
        jnp.einsum(
            "cln,chpn->clhp",
            read_state,
            arriving.astype(jnp.bfloat16),
            preferred_element_type=jnp.float32,
        )
        * carry_decay[:, :, :, None]
    )
    result = (
        within_stretch + from_before + skip_gain[None, None, :, None] * values.astype(jnp.float32)
    )
    ssm_rows = result.reshape(block_rows, local_width).astype(jnp.bfloat16)
    end_weight = ends_mask.astype(jnp.float32)
    has_end = jnp.sum(end_weight, axis=1)
    end_decay = jnp.sum(decay_heads * end_weight[:, None, :], axis=2)
    end_ids = jnp.sum(jnp.where(ends_mask, stretch_ids, 0), axis=1)
    keep_end = ((stretch_ids == end_ids[:, None]) & (has_end[:, None] > 0))[:, None, :]
    end_coef = (
        jnp.where(keep_end, jnp.exp(jnp.minimum(end_decay[:, :, None] - decay_heads, 0.0)), 0.0)
        * step_heads
    )
    end_rows = (values.astype(jnp.float32) * jnp.swapaxes(end_coef, 1, 2)[:, :, :, None]).astype(
        jnp.bfloat16
    )
    end_states = jnp.einsum(
        "clhp,cln->chpn", end_rows, write_state, preferred_element_type=jnp.float32
    )
    end_carry = (
        jnp.exp(end_decay) * ((end_ids == prior_ids) & (has_end > 0)).astype(jnp.float32)[:, None]
    )
    end_states = end_states + end_carry[:, :, None, None] * arriving
    final_block = jnp.sum(end_states, axis=0)[None]
    y_tokens = lax.all_to_all(
        ssm_rows.reshape(groups, sub_rows, local_width), "head", 0, 2, tiled=True
    ).reshape(sub_rows, inner_width)
    token_rows = (y_tokens.astype(jnp.float32), gates_tokens.astype(jnp.float32))
    gated = token_rows[0] * jax.nn.silu(token_rows[1])
    mean_square = jnp.mean(gated * gated, axis=1)
    scaled = gated * lax.rsqrt(mean_square + epsilon)[:, None] * norm_gain[None, :]
    gated_out = scaled.astype(jnp.bfloat16)
    return (gated_out, final_block)


def solution(mesh):
    seq_size, head_size = mesh.devices.shape
    fine = Mesh(mesh.devices.reshape(4, seq_size // 8, 2, head_size), SEQ + ("head",))
    in_specs = (
        P(SEQ + ("head",), None),
        P(SEQ, "head"),
        P(SEQ, "head"),
        P(SEQ, "head"),
        P(SEQ, None),
        P(),
        P(),
        P("head"),
        P("head"),
        P("head"),
        P(),
        P(),
    )
    out_specs = (P(SEQ + ("head",), None), P(SEQ, "head", None, None))
    return jax.shard_map(
        on_device, mesh=fine, in_specs=in_specs, out_specs=out_specs, check_vma=False
    )
```

```python
import jax
import jax.numpy as jnp
from jax import lax
from jax.sharding import Mesh, PartitionSpec as P

STRETCH = 256
SEQ = ("x", "z", "c")


epsilon = 1e-05


def from_behind(block, axis, distance):
    devices = range(lax.psum(1, axis))
    route = [(i - distance, i) for i in devices if i - distance in devices]
    return lax.ppermute(block, axis, route)


def segments_at(positions, prompt_ends):
    counted = jnp.sum((prompt_ends[None, :] <= positions[:, None]).astype(jnp.int32), axis=1)
    return jnp.where(positions < 0, -1, counted)


def on_device(
    hidden,
    w_values,
    w_gates,
    w_steps,
    w_states,
    conv_weight,
    conv_bias,
    step_bias,
    decay_rate,
    skip_gain,
    norm_gain,
    lengths,
):
    groups = lax.axis_size("head")
    group_index = lax.axis_index("head")
    block_index = lax.axis_index(SEQ)
    local_width = w_values.shape[1]
    inner_width = local_width * groups
    local_heads = decay_rate.shape[0]
    head_width = local_width // local_heads
    state_width = w_states.shape[1] // 2
    conv_taps = conv_weight.shape[0]
    prompt_ends = jnp.cumsum(lengths)
    block_hidden = lax.all_to_all(
        jnp.broadcast_to(hidden[None], (groups,) + hidden.shape), "head", 0, 0, tiled=True
    ).reshape(groups * hidden.shape[0], hidden.shape[1])
    block_rows = block_hidden.shape[0]
    sub_rows = block_rows // groups
    step_width = w_steps.shape[1]
    merged = jnp.concatenate([w_values, w_states, w_gates, w_steps], axis=1)
    shard_rows = merged.shape[0]
    padded_rows = -(-shard_rows // 16) * 16
    half = local_width + 2 * state_width
    merged = jnp.pad(merged, ((0, padded_rows - shard_rows), (0, 2 * half - merged.shape[1])))
    halves = jnp.stack([merged[:, :half], merged[:, half:]])
    own_half = lax.all_to_all(halves, "c", 0, 0, tiled=True).reshape(2 * padded_rows, half)
    own_half = lax.all_gather(own_half, "x", axis=0, tiled=True)
    block_hidden, own_half = lax.optimization_barrier((block_hidden, own_half))
    own_half = lax.all_gather(own_half, "z", axis=0, tiled=True)
    other_half = lax.ppermute(own_half, "c", [(0, 1), (1, 0)])
    x_size = lax.psum(1, "x")
    z_size = lax.psum(1, "z")
    c_size = lax.psum(1, "c")
    core_index = lax.axis_index("c")

    def spread_rows(rows):
        count = rows.shape[0]
        split = rows.reshape(count, x_size, z_size, c_size, shard_rows)
        split = jnp.pad(split, ((0, 0), (0, 0), (0, 0), (0, 0), (0, padded_rows - shard_rows)))
        split = jnp.transpose(split, (0, 2, 1, 3, 4))
        return split.reshape(count, x_size * z_size * c_size * padded_rows)

    rim_hidden = from_behind(block_hidden[block_rows - (conv_taps - 1) :], SEQ, 1)
    rim_count = rim_hidden.shape[0]
    both_rows = jnp.concatenate(
        [block_hidden, rim_hidden, jnp.zeros((8 - rim_count, block_hidden.shape[1]), jnp.bfloat16)]
    )
    spread = spread_rows(both_rows)
    with_own = jnp.dot(spread, own_half, preferred_element_type=jnp.float32)
    with_other = jnp.dot(spread, other_half, preferred_element_type=jnp.float32)
    first_cols = jnp.where(core_index == 0, with_own, with_other)
    second_cols = jnp.where(core_index == 0, with_other, with_own)
    projected = jnp.concatenate([first_cols, second_cols], axis=1)
    conv_end = local_width + 2 * state_width
    prior_rim = projected[block_rows : block_rows + rim_count, :conv_end].astype(jnp.bfloat16)
    projected = projected[:block_rows]
    pre_rows = projected[:, :conv_end].astype(jnp.bfloat16)
    gates_sum = projected[:, conv_end : conv_end + local_width]
    steps_sum = projected[:, conv_end + local_width : conv_end + local_width + step_width]
    head_gates = gates_sum.astype(jnp.bfloat16)
    gates_tokens = lax.all_to_all(
        head_gates.reshape(groups, sub_rows, local_width), "head", 0, 2, tiled=True
    ).reshape(sub_rows, inner_width)
    local_taps = jnp.concatenate(
        [
            lax.dynamic_slice_in_dim(conv_weight, group_index * local_width, local_width, 1),
            conv_weight[:, inner_width:],
        ],
        axis=1,
    )
    local_bias = jnp.concatenate(
        [
            lax.dynamic_slice_in_dim(conv_bias, group_index * local_width, local_width, 0),
            conv_bias[inner_width:],
        ],
        axis=0,
    )
    block_start = block_index * block_rows
    extended = jnp.concatenate([prior_rim, pre_rows], axis=0)
    ext_positions = (
        block_start - (conv_taps - 1) + jnp.arange(block_rows + conv_taps - 1, dtype=jnp.int32)
    )
    ext_ids = segments_at(ext_positions, prompt_ends)
    own_ids = ext_ids[conv_taps - 1 :]
    filtered = jnp.zeros(pre_rows.shape, jnp.float32) + local_bias[None, :]
    for offset in range(conv_taps):
        matches = (ext_ids[offset : offset + block_rows] == own_ids).astype(jnp.float32)
        filtered = (
            filtered
            + local_taps[offset][None, :]
            * extended[offset : offset + block_rows].astype(jnp.float32)
            * matches[:, None]
        )
    conv_out = jax.nn.silu(filtered).astype(jnp.bfloat16)
    head_values = conv_out[:, :local_width]
    both_states = conv_out[:, local_width:]
    stretch_rows = STRETCH
    stretches = block_rows // stretch_rows
    positions = block_start + jnp.arange(block_rows, dtype=jnp.int32)
    segment_ids = segments_at(positions, prompt_ends)
    next_ids = segments_at(positions + 1, prompt_ends)
    before_ids = segments_at(positions - 1, prompt_ends)
    stretch_ids = segment_ids.reshape(stretches, stretch_rows)
    prior_ids = before_ids.reshape(stretches, stretch_rows)[:, 0]
    ends_mask = (segment_ids != next_ids).reshape(stretches, stretch_rows)
    step_sizes = jax.nn.softplus(steps_sum + step_bias[None, :])
    decay_steps = step_sizes * decay_rate[None, :]
    log_decay = -jnp.cumsum(decay_steps.reshape(stretches, stretch_rows, local_heads), axis=1)
    decay_heads = jnp.swapaxes(log_decay, 1, 2)
    step_heads = jnp.swapaxes(step_sizes.reshape(stretches, stretch_rows, local_heads), 1, 2)
    values = head_values.reshape(stretches, stretch_rows, local_heads, head_width)
    write_state = both_states[:, :state_width].reshape(stretches, stretch_rows, state_width)
    read_state = both_states[:, state_width:].reshape(stretches, stretch_rows, state_width)
    intersection = jnp.einsum(
        "ctn,csn->cts", read_state, write_state, preferred_element_type=jnp.float32
    )
    token_order = jnp.arange(stretch_rows, dtype=jnp.int32)
    causal = token_order[:, None] >= token_order[None, :]
    allowed = causal[None] & (stretch_ids[:, :, None] == stretch_ids[:, None, :])
    spread = decay_heads[:, :, :, None] - decay_heads[:, :, None, :]
    weights = (
        jnp.where(allowed[:, None], jnp.exp(jnp.minimum(spread, 0.0)), 0.0)
        * step_heads[:, :, None, :]
    )
    scores = (intersection[:, None] * weights).astype(jnp.bfloat16)
    within_stretch = jnp.einsum(
        "chts,cshp->cthp", scores, values, preferred_element_type=jnp.float32
    )
    last_ids = stretch_ids[:, -1]
    tail_decay = decay_heads[:, :, -1:]
    keep_tail = (stretch_ids == last_ids[:, None])[:, None, :]
    tail_coef = (
        jnp.where(keep_tail, jnp.exp(jnp.minimum(tail_decay - decay_heads, 0.0)), 0.0) * step_heads
    )
    tail_rows = (values.astype(jnp.float32) * jnp.swapaxes(tail_coef, 1, 2)[:, :, :, None]).astype(
        jnp.bfloat16
    )
    stretch_states = jnp.einsum(
        "clhp,cln->chpn", tail_rows, write_state, preferred_element_type=jnp.float32
    )
    stretch_gates = (
        jnp.exp(decay_heads[:, :, -1]) * (last_ids == prior_ids).astype(jnp.float32)[:, None]
    )
    own_gate = jnp.broadcast_to(stretch_gates[0][:, None, None], (local_heads, 8, state_width))
    packed = jnp.concatenate([stretch_states[0], own_gate], axis=1).astype(jnp.bfloat16)
    p1 = from_behind(packed, SEQ, 1)
    p2 = from_behind(packed, SEQ, 2)
    p3 = from_behind(packed, SEQ, 3)
    g1 = p1[:, head_width : head_width + 1, :1]
    g2 = p2[:, head_width : head_width + 1, :1]
    p1, p2, p3, g1, g2 = (part.astype(jnp.float32) for part in (p1, p2, p3, g1, g2))
    incoming = p1[:, :head_width] + g1 * (p2[:, :head_width] + g2 * p3[:, :head_width])
    arriving = incoming[None]
    carry_mask = (stretch_ids == prior_ids[:, None]).astype(jnp.float32)
    carry_decay = jnp.exp(log_decay) * carry_mask[:, :, None]
    from_before = (
        jnp.einsum(
            "cln,chpn->clhp",
            read_state,
            arriving.astype(jnp.bfloat16),
            preferred_element_type=jnp.float32,
        )
        * carry_decay[:, :, :, None]
    )
    result = (
        within_stretch + from_before + skip_gain[None, None, :, None] * values.astype(jnp.float32)
    )
    ssm_rows = result.reshape(block_rows, local_width).astype(jnp.bfloat16)
    end_weight = ends_mask.astype(jnp.float32)
    has_end = jnp.sum(end_weight, axis=1)
    end_decay = jnp.sum(decay_heads * end_weight[:, None, :], axis=2)
    end_ids = jnp.sum(jnp.where(ends_mask, stretch_ids, 0), axis=1)
    keep_end = ((stretch_ids == end_ids[:, None]) & (has_end[:, None] > 0))[:, None, :]
    end_coef = (
        jnp.where(keep_end, jnp.exp(jnp.minimum(end_decay[:, :, None] - decay_heads, 0.0)), 0.0)
        * step_heads
    )
    end_rows = (values.astype(jnp.float32) * jnp.swapaxes(end_coef, 1, 2)[:, :, :, None]).astype(
        jnp.bfloat16
    )
    end_states = jnp.einsum(
        "clhp,cln->chpn", end_rows, write_state, preferred_element_type=jnp.float32
    )
    end_carry = (
        jnp.exp(end_decay) * ((end_ids == prior_ids) & (has_end > 0)).astype(jnp.float32)[:, None]
    )
    end_states = end_states + end_carry[:, :, None, None] * arriving
    final_block = jnp.sum(end_states, axis=0)[None]
    y_tokens = lax.all_to_all(
        ssm_rows.reshape(groups, sub_rows, local_width), "head", 0, 2, tiled=True
    ).reshape(sub_rows, inner_width)
    token_rows = (y_tokens.astype(jnp.float32), gates_tokens.astype(jnp.float32))
    gated = token_rows[0] * jax.nn.silu(token_rows[1])
    mean_square = jnp.mean(gated * gated, axis=1)
    scaled = gated * lax.rsqrt(mean_square + epsilon)[:, None] * norm_gain[None, :]
    gated_out = scaled.astype(jnp.bfloat16)
    return (gated_out, final_block)


def solution(mesh):
    seq_size, head_size = mesh.devices.shape
    fine = Mesh(mesh.devices.reshape(4, seq_size // 8, 2, head_size), SEQ + ("head",))
    in_specs = (
        P(SEQ + ("head",), None),
        P(SEQ, "head"),
        P(SEQ, "head"),
        P(SEQ, "head"),
        P(SEQ, None),
        P(),
        P(),
        P("head"),
        P("head"),
        P("head"),
        P(),
        P(),
    )
    out_specs = (P(SEQ + ("head",), None), P(SEQ, "head", None, None))
    return jax.shard_map(
        on_device, mesh=fine, in_specs=in_specs, out_specs=out_specs, check_vma=False
    )
```

```python
import jax
import jax.numpy as jnp
from jax import lax
from jax.sharding import Mesh, PartitionSpec as P

STRETCH = 256
SEQ = ("x", "z", "c")


epsilon = 1e-05


def from_behind(block, axis, distance):
    devices = range(lax.psum(1, axis))
    route = [(i - distance, i) for i in devices if i - distance in devices]
    return lax.ppermute(block, axis, route)


def segments_at(positions, prompt_ends):
    counted = jnp.sum((prompt_ends[None, :] <= positions[:, None]).astype(jnp.int32), axis=1)
    return jnp.where(positions < 0, -1, counted)


def on_device(
    hidden,
    w_values,
    w_gates,
    w_steps,
    w_states,
    conv_weight,
    conv_bias,
    step_bias,
    decay_rate,
    skip_gain,
    norm_gain,
    lengths,
):
    groups = lax.axis_size("head")
    group_index = lax.axis_index("head")
    block_index = lax.axis_index(SEQ)
    local_width = w_values.shape[1]
    inner_width = local_width * groups
    local_heads = decay_rate.shape[0]
    head_width = local_width // local_heads
    state_width = w_states.shape[1] // 2
    conv_taps = conv_weight.shape[0]
    prompt_ends = jnp.cumsum(lengths)
    block_hidden = lax.all_to_all(
        jnp.broadcast_to(hidden[None], (groups,) + hidden.shape), "head", 0, 0, tiled=True
    ).reshape(groups * hidden.shape[0], hidden.shape[1])
    block_rows = block_hidden.shape[0]
    sub_rows = block_rows // groups
    step_width = w_steps.shape[1]
    merged = jnp.concatenate([w_values, w_states, w_gates, w_steps], axis=1)
    shard_rows = merged.shape[0]
    padded_rows = -(-shard_rows // 16) * 16
    half = local_width + 2 * state_width
    merged = jnp.pad(merged, ((0, padded_rows - shard_rows), (0, 2 * half - merged.shape[1])))
    halves = jnp.stack([merged[:, :half], merged[:, half:]])
    own_half = lax.all_to_all(halves, "c", 0, 0, tiled=True).reshape(2 * padded_rows, half)
    own_half = lax.all_gather(own_half, "x", axis=0, tiled=True)
    x_size = lax.psum(1, "x")
    z_size = lax.psum(1, "z")
    c_size = lax.psum(1, "c")
    core_index = lax.axis_index("c")
    is_first = core_index == 0
    swap = [(0, 1), (1, 0)]

    def spread_rows(rows):
        count = rows.shape[0]
        split = rows.reshape(count, x_size, z_size, c_size, shard_rows)
        split = jnp.pad(split, ((0, 0), (0, 0), (0, 0), (0, 0), (0, padded_rows - shard_rows)))
        split = jnp.transpose(split, (0, 2, 1, 3, 4))
        return split.reshape(count, x_size * z_size * c_size * padded_rows)

    last_rows = block_hidden[block_rows - (conv_taps - 1) :]
    rim_count = last_rows.shape[0]
    rim_near = from_behind(last_rows, SEQ, 1)
    rim_far = from_behind(last_rows, SEQ, 2)
    partner_block = lax.ppermute(block_hidden, "c", swap)
    filler = jnp.zeros((8 - rim_count, block_hidden.shape[1]), jnp.bfloat16)
    chip_rows = jnp.concatenate(
        [
            jnp.where(is_first, block_hidden, partner_block),
            jnp.where(is_first, rim_near, rim_far),
            filler,
            jnp.where(is_first, partner_block, block_hidden),
            jnp.where(is_first, last_rows, rim_near),
            filler,
        ]
    )
    spread, own_half = lax.optimization_barrier((spread_rows(chip_rows), own_half))
    own_half = lax.all_gather(own_half, "z", axis=0, tiled=True)
    core_rows = block_rows + 8
    results = jnp.dot(spread, own_half, preferred_element_type=jnp.float32)
    own_rows = lax.dynamic_slice_in_dim(results, core_index * core_rows, core_rows, 0)
    partner_rows = lax.dynamic_slice_in_dim(results, (1 - core_index) * core_rows, core_rows, 0)
    sent_narrow, sent_wide = lax.ppermute(
        (partner_rows.astype(jnp.bfloat16), partner_rows[:, local_width : local_width + 128]),
        "c",
        swap,
    )
    conv_part = jnp.where(is_first, own_rows.astype(jnp.bfloat16), sent_narrow)
    gate_part = jnp.where(
        is_first, sent_narrow[:, :local_width], own_rows[:, :local_width].astype(jnp.bfloat16)
    )
    step_part = jnp.where(
        is_first, sent_wide[:, :step_width], own_rows[:, local_width : local_width + step_width]
    )
    conv_end = local_width + 2 * state_width
    prior_rim = conv_part[block_rows : block_rows + rim_count]
    pre_rows = conv_part[:block_rows]
    gates_sum = gate_part[:block_rows]
    steps_sum = step_part[:block_rows]
    head_gates = gates_sum.astype(jnp.bfloat16)
    gates_tokens = lax.all_to_all(
        head_gates.reshape(groups, sub_rows, local_width), "head", 0, 2, tiled=True
    ).reshape(sub_rows, inner_width)
    local_taps = jnp.concatenate(
        [
            lax.dynamic_slice_in_dim(conv_weight, group_index * local_width, local_width, 1),
            conv_weight[:, inner_width:],
        ],
        axis=1,
    )
    local_bias = jnp.concatenate(
        [
            lax.dynamic_slice_in_dim(conv_bias, group_index * local_width, local_width, 0),
            conv_bias[inner_width:],
        ],
        axis=0,
    )
    block_start = block_index * block_rows
    extended = jnp.concatenate([prior_rim, pre_rows], axis=0)
    ext_positions = (
        block_start - (conv_taps - 1) + jnp.arange(block_rows + conv_taps - 1, dtype=jnp.int32)
    )
    ext_ids = segments_at(ext_positions, prompt_ends)
    own_ids = ext_ids[conv_taps - 1 :]
    filtered = jnp.zeros(pre_rows.shape, jnp.float32) + local_bias[None, :]
    for offset in range(conv_taps):
        matches = (ext_ids[offset : offset + block_rows] == own_ids).astype(jnp.float32)
        filtered = (
            filtered
            + local_taps[offset][None, :]
            * extended[offset : offset + block_rows].astype(jnp.float32)
            * matches[:, None]
        )
    conv_out = jax.nn.silu(filtered).astype(jnp.bfloat16)
    head_values = conv_out[:, :local_width]
    both_states = conv_out[:, local_width:]
    stretch_rows = STRETCH
    stretches = block_rows // stretch_rows
    positions = block_start + jnp.arange(block_rows, dtype=jnp.int32)
    segment_ids = segments_at(positions, prompt_ends)
    next_ids = segments_at(positions + 1, prompt_ends)
    before_ids = segments_at(positions - 1, prompt_ends)
    stretch_ids = segment_ids.reshape(stretches, stretch_rows)
    prior_ids = before_ids.reshape(stretches, stretch_rows)[:, 0]
    ends_mask = (segment_ids != next_ids).reshape(stretches, stretch_rows)
    step_sizes = jax.nn.softplus(steps_sum + step_bias[None, :])
    decay_steps = step_sizes * decay_rate[None, :]
    log_decay = -jnp.cumsum(decay_steps.reshape(stretches, stretch_rows, local_heads), axis=1)
    decay_heads = jnp.swapaxes(log_decay, 1, 2)
    step_heads = jnp.swapaxes(step_sizes.reshape(stretches, stretch_rows, local_heads), 1, 2)
    values = head_values.reshape(stretches, stretch_rows, local_heads, head_width)
    write_state = both_states[:, :state_width].reshape(stretches, stretch_rows, state_width)
    read_state = both_states[:, state_width:].reshape(stretches, stretch_rows, state_width)
    intersection = jnp.einsum(
        "ctn,csn->cts", read_state, write_state, preferred_element_type=jnp.float32
    )
    token_order = jnp.arange(stretch_rows, dtype=jnp.int32)
    causal = token_order[:, None] >= token_order[None, :]
    allowed = causal[None] & (stretch_ids[:, :, None] == stretch_ids[:, None, :])
    spread = decay_heads[:, :, :, None] - decay_heads[:, :, None, :]
    weights = (
        jnp.where(allowed[:, None], jnp.exp(jnp.minimum(spread, 0.0)), 0.0)
        * step_heads[:, :, None, :]
    )
    scores = (intersection[:, None] * weights).astype(jnp.bfloat16)
    within_stretch = jnp.einsum(
        "chts,cshp->cthp", scores, values, preferred_element_type=jnp.float32
    )
    last_ids = stretch_ids[:, -1]
    tail_decay = decay_heads[:, :, -1:]
    keep_tail = (stretch_ids == last_ids[:, None])[:, None, :]
    tail_coef = (
        jnp.where(keep_tail, jnp.exp(jnp.minimum(tail_decay - decay_heads, 0.0)), 0.0) * step_heads
    )
    tail_rows = (values.astype(jnp.float32) * jnp.swapaxes(tail_coef, 1, 2)[:, :, :, None]).astype(
        jnp.bfloat16
    )
    stretch_states = jnp.einsum(
        "clhp,cln->chpn", tail_rows, write_state, preferred_element_type=jnp.float32
    )
    stretch_gates = (
        jnp.exp(decay_heads[:, :, -1]) * (last_ids == prior_ids).astype(jnp.float32)[:, None]
    )
    own_gate = jnp.broadcast_to(stretch_gates[0][:, None, None], (local_heads, 8, state_width))
    packed = jnp.concatenate([stretch_states[0], own_gate], axis=1).astype(jnp.bfloat16)
    p1 = from_behind(packed, SEQ, 1)
    p2 = from_behind(packed, SEQ, 2)
    p3 = from_behind(packed, SEQ, 3)
    g1 = p1[:, head_width : head_width + 1, :1]
    g2 = p2[:, head_width : head_width + 1, :1]
    p1, p2, p3, g1, g2 = (part.astype(jnp.float32) for part in (p1, p2, p3, g1, g2))
    incoming = p1[:, :head_width] + g1 * (p2[:, :head_width] + g2 * p3[:, :head_width])
    arriving = incoming[None]
    carry_mask = (stretch_ids == prior_ids[:, None]).astype(jnp.float32)
    carry_decay = jnp.exp(log_decay) * carry_mask[:, :, None]
    from_before = (
        jnp.einsum(
            "cln,chpn->clhp",
            read_state,
            arriving.astype(jnp.bfloat16),
            preferred_element_type=jnp.float32,
        )
        * carry_decay[:, :, :, None]
    )
    result = (
        within_stretch + from_before + skip_gain[None, None, :, None] * values.astype(jnp.float32)
    )
    ssm_rows = result.reshape(block_rows, local_width).astype(jnp.bfloat16)
    end_weight = ends_mask.astype(jnp.float32)
    has_end = jnp.sum(end_weight, axis=1)
    end_decay = jnp.sum(decay_heads * end_weight[:, None, :], axis=2)
    end_ids = jnp.sum(jnp.where(ends_mask, stretch_ids, 0), axis=1)
    keep_end = ((stretch_ids == end_ids[:, None]) & (has_end[:, None] > 0))[:, None, :]
    end_coef = (
        jnp.where(keep_end, jnp.exp(jnp.minimum(end_decay[:, :, None] - decay_heads, 0.0)), 0.0)
        * step_heads
    )
    end_rows = (values.astype(jnp.float32) * jnp.swapaxes(end_coef, 1, 2)[:, :, :, None]).astype(
        jnp.bfloat16
    )
    end_states = jnp.einsum(
        "clhp,cln->chpn", end_rows, write_state, preferred_element_type=jnp.float32
    )
    end_carry = (
        jnp.exp(end_decay) * ((end_ids == prior_ids) & (has_end > 0)).astype(jnp.float32)[:, None]
    )
    end_states = end_states + end_carry[:, :, None, None] * arriving
    final_block = jnp.sum(end_states, axis=0)[None]
    y_tokens = lax.all_to_all(
        ssm_rows.reshape(groups, sub_rows, local_width), "head", 0, 2, tiled=True
    ).reshape(sub_rows, inner_width)
    token_rows = (y_tokens.astype(jnp.float32), gates_tokens.astype(jnp.float32))
    gated = token_rows[0] * jax.nn.silu(token_rows[1])
    mean_square = jnp.mean(gated * gated, axis=1)
    scaled = gated * lax.rsqrt(mean_square + epsilon)[:, None] * norm_gain[None, :]
    gated_out = scaled.astype(jnp.bfloat16)
    return (gated_out, final_block)


def solution(mesh):
    seq_size, head_size = mesh.devices.shape
    fine = Mesh(mesh.devices.reshape(4, seq_size // 8, 2, head_size), SEQ + ("head",))
    in_specs = (
        P(SEQ + ("head",), None),
        P(SEQ, "head"),
        P(SEQ, "head"),
        P(SEQ, "head"),
        P(SEQ, None),
        P(),
        P(),
        P("head"),
        P("head"),
        P("head"),
        P(),
        P(),
    )
    out_specs = (P(SEQ + ("head",), None), P(SEQ, "head", None, None))
    return jax.shard_map(
        on_device, mesh=fine, in_specs=in_specs, out_specs=out_specs, check_vma=False
    )
```

```python
import jax
import jax.numpy as jnp
from jax import lax
from jax.sharding import Mesh, PartitionSpec as P

STRETCH = 256
SEQ = ("x", "z", "c")


epsilon = 1e-05


def from_behind(block, axis, distance):
    devices = range(lax.psum(1, axis))
    route = [(i - distance, i) for i in devices if i - distance in devices]
    return lax.ppermute(block, axis, route)


def segments_at(positions, prompt_ends):
    counted = jnp.sum((prompt_ends[None, :] <= positions[:, None]).astype(jnp.int32), axis=1)
    return jnp.where(positions < 0, -1, counted)


def on_device(
    hidden,
    w_values,
    w_gates,
    w_steps,
    w_states,
    conv_weight,
    conv_bias,
    step_bias,
    decay_rate,
    skip_gain,
    norm_gain,
    lengths,
):
    groups = lax.axis_size("head")
    group_index = lax.axis_index("head")
    block_index = lax.axis_index(SEQ)
    local_width = w_values.shape[1]
    inner_width = local_width * groups
    local_heads = decay_rate.shape[0]
    head_width = local_width // local_heads
    state_width = w_states.shape[1] // 2
    conv_taps = conv_weight.shape[0]
    prompt_ends = jnp.cumsum(lengths)
    block_hidden = lax.all_to_all(
        jnp.broadcast_to(hidden[None], (groups,) + hidden.shape), "head", 0, 0, tiled=True
    ).reshape(groups * hidden.shape[0], hidden.shape[1])
    block_rows = block_hidden.shape[0]
    sub_rows = block_rows // groups
    step_width = w_steps.shape[1]
    merged = jnp.concatenate([w_values, w_states, w_gates, w_steps], axis=1)
    shard_rows = merged.shape[0]
    padded_rows = -(-shard_rows // 16) * 16
    half = local_width + 2 * state_width
    merged = jnp.pad(merged, ((0, padded_rows - shard_rows), (0, 2 * half - merged.shape[1])))
    halves = jnp.stack([merged[:, :half], merged[:, half:]])
    own_half = lax.all_to_all(halves, "c", 0, 0, tiled=True).reshape(2 * padded_rows, half)
    own_half = lax.all_gather(own_half, "x", axis=0, tiled=True)
    x_size = lax.psum(1, "x")
    z_size = lax.psum(1, "z")
    c_size = lax.psum(1, "c")
    core_index = lax.axis_index("c")
    is_first = core_index == 0
    swap = [(0, 1), (1, 0)]

    def spread_rows(rows):
        count = rows.shape[0]
        split = rows.reshape(count, x_size, z_size, c_size, shard_rows)
        split = jnp.pad(split, ((0, 0), (0, 0), (0, 0), (0, 0), (0, padded_rows - shard_rows)))
        split = jnp.transpose(split, (0, 2, 1, 3, 4))
        return split.reshape(count, x_size * z_size * c_size * padded_rows)

    last_rows = block_hidden[block_rows - (conv_taps - 1) :]
    rim_count = last_rows.shape[0]
    rim_hidden = from_behind(last_rows, SEQ, 1)
    filler = jnp.zeros((8 - rim_count, block_hidden.shape[1]), jnp.bfloat16)
    own_spread = spread_rows(jnp.concatenate([block_hidden, rim_hidden, filler]))
    partner_spread = lax.ppermute(own_spread, "c", swap)
    own_spread, partner_spread, own_half = lax.optimization_barrier(
        (own_spread, partner_spread, own_half)
    )
    own_half = lax.all_gather(own_half, "z", axis=0, tiled=True)
    own_rows = jnp.dot(own_spread, own_half, preferred_element_type=jnp.float32)
    partner_rows = jnp.dot(partner_spread, own_half, preferred_element_type=jnp.float32)
    sent_narrow, sent_wide = lax.ppermute(
        (partner_rows.astype(jnp.bfloat16), partner_rows[:, local_width : local_width + 128]),
        "c",
        swap,
    )
    conv_part = jnp.where(is_first, own_rows.astype(jnp.bfloat16), sent_narrow)
    gate_part = jnp.where(
        is_first, sent_narrow[:, :local_width], own_rows[:, :local_width].astype(jnp.bfloat16)
    )
    step_part = jnp.where(
        is_first, sent_wide[:, :step_width], own_rows[:, local_width : local_width + step_width]
    )
    conv_end = local_width + 2 * state_width
    prior_rim = conv_part[block_rows : block_rows + rim_count]
    pre_rows = conv_part[:block_rows]
    gates_sum = gate_part[:block_rows]
    steps_sum = step_part[:block_rows]
    head_gates = gates_sum.astype(jnp.bfloat16)
    gates_tokens = lax.all_to_all(
        head_gates.reshape(groups, sub_rows, local_width), "head", 0, 2, tiled=True
    ).reshape(sub_rows, inner_width)
    local_taps = jnp.concatenate(
        [
            lax.dynamic_slice_in_dim(conv_weight, group_index * local_width, local_width, 1),
            conv_weight[:, inner_width:],
        ],
        axis=1,
    )
    local_bias = jnp.concatenate(
        [
            lax.dynamic_slice_in_dim(conv_bias, group_index * local_width, local_width, 0),
            conv_bias[inner_width:],
        ],
        axis=0,
    )
    block_start = block_index * block_rows
    extended = jnp.concatenate([prior_rim, pre_rows], axis=0)
    ext_positions = (
        block_start - (conv_taps - 1) + jnp.arange(block_rows + conv_taps - 1, dtype=jnp.int32)
    )
    ext_ids = segments_at(ext_positions, prompt_ends)
    own_ids = ext_ids[conv_taps - 1 :]
    filtered = jnp.zeros(pre_rows.shape, jnp.float32) + local_bias[None, :]
    for offset in range(conv_taps):
        matches = (ext_ids[offset : offset + block_rows] == own_ids).astype(jnp.float32)
        filtered = (
            filtered
            + local_taps[offset][None, :]
            * extended[offset : offset + block_rows].astype(jnp.float32)
            * matches[:, None]
        )
    conv_out = jax.nn.silu(filtered).astype(jnp.bfloat16)
    head_values = conv_out[:, :local_width]
    both_states = conv_out[:, local_width:]
    stretch_rows = STRETCH
    stretches = block_rows // stretch_rows
    positions = block_start + jnp.arange(block_rows, dtype=jnp.int32)
    segment_ids = segments_at(positions, prompt_ends)
    next_ids = segments_at(positions + 1, prompt_ends)
    before_ids = segments_at(positions - 1, prompt_ends)
    stretch_ids = segment_ids.reshape(stretches, stretch_rows)
    prior_ids = before_ids.reshape(stretches, stretch_rows)[:, 0]
    ends_mask = (segment_ids != next_ids).reshape(stretches, stretch_rows)
    step_sizes = jax.nn.softplus(steps_sum + step_bias[None, :])
    decay_steps = step_sizes * decay_rate[None, :]
    log_decay = -jnp.cumsum(decay_steps.reshape(stretches, stretch_rows, local_heads), axis=1)
    decay_heads = jnp.swapaxes(log_decay, 1, 2)
    step_heads = jnp.swapaxes(step_sizes.reshape(stretches, stretch_rows, local_heads), 1, 2)
    values = head_values.reshape(stretches, stretch_rows, local_heads, head_width)
    write_state = both_states[:, :state_width].reshape(stretches, stretch_rows, state_width)
    read_state = both_states[:, state_width:].reshape(stretches, stretch_rows, state_width)
    intersection = jnp.einsum(
        "ctn,csn->cts", read_state, write_state, preferred_element_type=jnp.float32
    )
    token_order = jnp.arange(stretch_rows, dtype=jnp.int32)
    causal = token_order[:, None] >= token_order[None, :]
    allowed = causal[None] & (stretch_ids[:, :, None] == stretch_ids[:, None, :])
    spread = decay_heads[:, :, :, None] - decay_heads[:, :, None, :]
    weights = (
        jnp.where(allowed[:, None], jnp.exp(jnp.minimum(spread, 0.0)), 0.0)
        * step_heads[:, :, None, :]
    )
    scores = (intersection[:, None] * weights).astype(jnp.bfloat16)
    within_stretch = jnp.einsum(
        "chts,cshp->cthp", scores, values, preferred_element_type=jnp.float32
    )
    last_ids = stretch_ids[:, -1]
    tail_decay = decay_heads[:, :, -1:]
    keep_tail = (stretch_ids == last_ids[:, None])[:, None, :]
    tail_coef = (
        jnp.where(keep_tail, jnp.exp(jnp.minimum(tail_decay - decay_heads, 0.0)), 0.0) * step_heads
    )
    tail_rows = (values.astype(jnp.float32) * jnp.swapaxes(tail_coef, 1, 2)[:, :, :, None]).astype(
        jnp.bfloat16
    )
    stretch_states = jnp.einsum(
        "clhp,cln->chpn", tail_rows, write_state, preferred_element_type=jnp.float32
    )
    stretch_gates = (
        jnp.exp(decay_heads[:, :, -1]) * (last_ids == prior_ids).astype(jnp.float32)[:, None]
    )
    own_gate = jnp.broadcast_to(stretch_gates[0][:, None, None], (local_heads, 8, state_width))
    packed = jnp.concatenate([stretch_states[0], own_gate], axis=1).astype(jnp.bfloat16)
    p1 = from_behind(packed, SEQ, 1)
    p2 = from_behind(packed, SEQ, 2)
    p3 = from_behind(packed, SEQ, 3)
    g1 = p1[:, head_width : head_width + 1, :1]
    g2 = p2[:, head_width : head_width + 1, :1]
    p1, p2, p3, g1, g2 = (part.astype(jnp.float32) for part in (p1, p2, p3, g1, g2))
    incoming = p1[:, :head_width] + g1 * (p2[:, :head_width] + g2 * p3[:, :head_width])
    arriving = incoming[None]
    carry_mask = (stretch_ids == prior_ids[:, None]).astype(jnp.float32)
    carry_decay = jnp.exp(log_decay) * carry_mask[:, :, None]
    from_before = (
        jnp.einsum(
            "cln,chpn->clhp",
            read_state,
            arriving.astype(jnp.bfloat16),
            preferred_element_type=jnp.float32,
        )
        * carry_decay[:, :, :, None]
    )
    result = (
        within_stretch + from_before + skip_gain[None, None, :, None] * values.astype(jnp.float32)
    )
    ssm_rows = result.reshape(block_rows, local_width).astype(jnp.bfloat16)
    end_weight = ends_mask.astype(jnp.float32)
    has_end = jnp.sum(end_weight, axis=1)
    end_decay = jnp.sum(decay_heads * end_weight[:, None, :], axis=2)
    end_ids = jnp.sum(jnp.where(ends_mask, stretch_ids, 0), axis=1)
    keep_end = ((stretch_ids == end_ids[:, None]) & (has_end[:, None] > 0))[:, None, :]
    end_coef = (
        jnp.where(keep_end, jnp.exp(jnp.minimum(end_decay[:, :, None] - decay_heads, 0.0)), 0.0)
        * step_heads
    )
    end_rows = (values.astype(jnp.float32) * jnp.swapaxes(end_coef, 1, 2)[:, :, :, None]).astype(
        jnp.bfloat16
    )
    end_states = jnp.einsum(
        "clhp,cln->chpn", end_rows, write_state, preferred_element_type=jnp.float32
    )
    end_carry = (
        jnp.exp(end_decay) * ((end_ids == prior_ids) & (has_end > 0)).astype(jnp.float32)[:, None]
    )
    end_states = end_states + end_carry[:, :, None, None] * arriving
    final_block = jnp.sum(end_states, axis=0)[None]
    y_tokens = lax.all_to_all(
        ssm_rows.reshape(groups, sub_rows, local_width), "head", 0, 2, tiled=True
    ).reshape(sub_rows, inner_width)
    token_rows = (y_tokens.astype(jnp.float32), gates_tokens.astype(jnp.float32))
    gated = token_rows[0] * jax.nn.silu(token_rows[1])
    mean_square = jnp.mean(gated * gated, axis=1)
    scaled = gated * lax.rsqrt(mean_square + epsilon)[:, None] * norm_gain[None, :]
    gated_out = scaled.astype(jnp.bfloat16)
    return (gated_out, final_block)


def solution(mesh):
    seq_size, head_size = mesh.devices.shape
    fine = Mesh(mesh.devices.reshape(4, seq_size // 8, 2, head_size), SEQ + ("head",))
    in_specs = (
        P(SEQ + ("head",), None),
        P(SEQ, "head"),
        P(SEQ, "head"),
        P(SEQ, "head"),
        P(SEQ, None),
        P(),
        P(),
        P("head"),
        P("head"),
        P("head"),
        P(),
        P(),
    )
    out_specs = (P(SEQ + ("head",), None), P(SEQ, "head", None, None))
    return jax.shard_map(
        on_device, mesh=fine, in_specs=in_specs, out_specs=out_specs, check_vma=False
    )
```

```python
import jax
import jax.numpy as jnp
from jax import lax
from jax.sharding import Mesh, PartitionSpec as P

STRETCH = 256
SEQ = ("x", "z", "c")


epsilon = 1e-05


def from_behind(block, axis, distance):
    devices = range(lax.psum(1, axis))
    route = [(i - distance, i) for i in devices if i - distance in devices]
    return lax.ppermute(block, axis, route)


def segments_at(positions, prompt_ends):
    counted = jnp.sum((prompt_ends[None, :] <= positions[:, None]).astype(jnp.int32), axis=1)
    return jnp.where(positions < 0, -1, counted)


def on_device(
    hidden,
    w_values,
    w_gates,
    w_steps,
    w_states,
    conv_weight,
    conv_bias,
    step_bias,
    decay_rate,
    skip_gain,
    norm_gain,
    lengths,
):
    groups = lax.axis_size("head")
    group_index = lax.axis_index("head")
    block_index = lax.axis_index(SEQ)
    local_width = w_values.shape[1]
    inner_width = local_width * groups
    local_heads = decay_rate.shape[0]
    head_width = local_width // local_heads
    state_width = w_states.shape[1] // 2
    conv_taps = conv_weight.shape[0]
    prompt_ends = jnp.cumsum(lengths)
    block_hidden = lax.all_to_all(
        jnp.broadcast_to(hidden[None], (groups,) + hidden.shape), "head", 0, 0, tiled=True
    ).reshape(groups * hidden.shape[0], hidden.shape[1])
    block_rows = block_hidden.shape[0]
    sub_rows = block_rows // groups
    step_width = w_steps.shape[1]
    merged = jnp.concatenate([w_values, w_states, w_gates, w_steps], axis=1)
    shard_rows = merged.shape[0]
    padded_rows = -(-shard_rows // 16) * 16
    half = local_width + 2 * state_width
    merged = jnp.pad(merged, ((0, padded_rows - shard_rows), (0, 2 * half - merged.shape[1])))
    halves = jnp.stack([merged[:, :half], merged[:, half:]])
    own_half = lax.all_to_all(halves, "c", 0, 0, tiled=True).reshape(2 * padded_rows, half)
    own_half = lax.all_gather(own_half, "x", axis=0, tiled=True)
    early_start = block_index * block_rows
    ext_positions = (
        early_start - (conv_taps - 1) + jnp.arange(block_rows + conv_taps - 1, dtype=jnp.int32)
    )
    positions = early_start + jnp.arange(block_rows, dtype=jnp.int32)
    early_ids = (
        segments_at(ext_positions, prompt_ends),
        segments_at(positions, prompt_ends),
        segments_at(positions + 1, prompt_ends),
        segments_at(positions - 1, prompt_ends),
    )
    block_hidden, own_half, early_ids = lax.optimization_barrier((block_hidden, own_half, early_ids))
    ext_ids, segment_ids, next_ids, before_ids = early_ids
    own_half = lax.all_gather(own_half, "z", axis=0, tiled=True)
    other_half = lax.ppermute(own_half, "c", [(0, 1), (1, 0)])
    x_size = lax.psum(1, "x")
    z_size = lax.psum(1, "z")
    c_size = lax.psum(1, "c")
    core_index = lax.axis_index("c")

    def spread_rows(rows):
        count = rows.shape[0]
        split = rows.reshape(count, x_size, z_size, c_size, shard_rows)
        split = jnp.pad(split, ((0, 0), (0, 0), (0, 0), (0, 0), (0, padded_rows - shard_rows)))
        split = jnp.transpose(split, (0, 2, 1, 3, 4))
        return split.reshape(count, x_size * z_size * c_size * padded_rows)

    rim_hidden = from_behind(block_hidden[block_rows - (conv_taps - 1) :], SEQ, 1)
    rim_count = rim_hidden.shape[0]
    both_rows = jnp.concatenate(
        [block_hidden, rim_hidden, jnp.zeros((8 - rim_count, block_hidden.shape[1]), jnp.bfloat16)]
    )
    spread = spread_rows(both_rows)
    with_own = jnp.dot(spread, own_half, preferred_element_type=jnp.float32)
    with_other = jnp.dot(spread, other_half, preferred_element_type=jnp.float32)
    first_cols = jnp.where(core_index == 0, with_own, with_other)
    second_cols = jnp.where(core_index == 0, with_other, with_own)
    projected = jnp.concatenate([first_cols, second_cols], axis=1)
    conv_end = local_width + 2 * state_width
    prior_rim = projected[block_rows : block_rows + rim_count, :conv_end].astype(jnp.bfloat16)
    projected = projected[:block_rows]
    pre_rows = projected[:, :conv_end].astype(jnp.bfloat16)
    gates_sum = projected[:, conv_end : conv_end + local_width]
    steps_sum = projected[:, conv_end + local_width : conv_end + local_width + step_width]
    head_gates = gates_sum.astype(jnp.bfloat16)
    gates_tokens = lax.all_to_all(
        head_gates.reshape(groups, sub_rows, local_width), "head", 0, 2, tiled=True
    ).reshape(sub_rows, inner_width)
    local_taps = jnp.concatenate(
        [
            lax.dynamic_slice_in_dim(conv_weight, group_index * local_width, local_width, 1),
            conv_weight[:, inner_width:],
        ],
        axis=1,
    )
    local_bias = jnp.concatenate(
        [
            lax.dynamic_slice_in_dim(conv_bias, group_index * local_width, local_width, 0),
            conv_bias[inner_width:],
        ],
        axis=0,
    )
    block_start = block_index * block_rows
    extended = jnp.concatenate([prior_rim, pre_rows], axis=0)
    own_ids = ext_ids[conv_taps - 1 :]
    filtered = jnp.zeros(pre_rows.shape, jnp.float32) + local_bias[None, :]
    for offset in range(conv_taps):
        matches = (ext_ids[offset : offset + block_rows] == own_ids).astype(jnp.float32)
        filtered = (
            filtered
            + local_taps[offset][None, :]
            * extended[offset : offset + block_rows].astype(jnp.float32)
            * matches[:, None]
        )
    conv_out = jax.nn.silu(filtered).astype(jnp.bfloat16)
    head_values = conv_out[:, :local_width]
    both_states = conv_out[:, local_width:]
    stretch_rows = STRETCH
    stretches = block_rows // stretch_rows
    stretch_ids = segment_ids.reshape(stretches, stretch_rows)
    prior_ids = before_ids.reshape(stretches, stretch_rows)[:, 0]
    ends_mask = (segment_ids != next_ids).reshape(stretches, stretch_rows)
    step_sizes = jax.nn.softplus(steps_sum + step_bias[None, :])
    decay_steps = step_sizes * decay_rate[None, :]
    log_decay = -jnp.cumsum(decay_steps.reshape(stretches, stretch_rows, local_heads), axis=1)
    decay_heads = jnp.swapaxes(log_decay, 1, 2)
    step_heads = jnp.swapaxes(step_sizes.reshape(stretches, stretch_rows, local_heads), 1, 2)
    values = head_values.reshape(stretches, stretch_rows, local_heads, head_width)
    write_state = both_states[:, :state_width].reshape(stretches, stretch_rows, state_width)
    read_state = both_states[:, state_width:].reshape(stretches, stretch_rows, state_width)
    intersection = jnp.einsum(
        "ctn,csn->cts", read_state, write_state, preferred_element_type=jnp.float32
    )
    token_order = jnp.arange(stretch_rows, dtype=jnp.int32)
    causal = token_order[:, None] >= token_order[None, :]
    allowed = causal[None] & (stretch_ids[:, :, None] == stretch_ids[:, None, :])
    spread = decay_heads[:, :, :, None] - decay_heads[:, :, None, :]
    weights = (
        jnp.where(allowed[:, None], jnp.exp(jnp.minimum(spread, 0.0)), 0.0)
        * step_heads[:, :, None, :]
    )
    scores = (intersection[:, None] * weights).astype(jnp.bfloat16)
    within_stretch = jnp.einsum(
        "chts,cshp->cthp", scores, values, preferred_element_type=jnp.float32
    )
    last_ids = stretch_ids[:, -1]
    tail_decay = decay_heads[:, :, -1:]
    keep_tail = (stretch_ids == last_ids[:, None])[:, None, :]
    tail_coef = (
        jnp.where(keep_tail, jnp.exp(jnp.minimum(tail_decay - decay_heads, 0.0)), 0.0) * step_heads
    )
    tail_rows = (values.astype(jnp.float32) * jnp.swapaxes(tail_coef, 1, 2)[:, :, :, None]).astype(
        jnp.bfloat16
    )
    stretch_states = jnp.einsum(
        "clhp,cln->chpn", tail_rows, write_state, preferred_element_type=jnp.float32
    )
    stretch_gates = (
        jnp.exp(decay_heads[:, :, -1]) * (last_ids == prior_ids).astype(jnp.float32)[:, None]
    )
    own_gate = jnp.broadcast_to(stretch_gates[0][:, None, None], (local_heads, 8, state_width))
    packed = jnp.concatenate([stretch_states[0], own_gate], axis=1).astype(jnp.bfloat16)
    p1 = from_behind(packed, SEQ, 1)
    p2 = from_behind(packed, SEQ, 2)
    p3 = from_behind(packed, SEQ, 3)
    g1 = p1[:, head_width : head_width + 1, :1]
    g2 = p2[:, head_width : head_width + 1, :1]
    p1, p2, p3, g1, g2 = (part.astype(jnp.float32) for part in (p1, p2, p3, g1, g2))
    incoming = p1[:, :head_width] + g1 * (p2[:, :head_width] + g2 * p3[:, :head_width])
    arriving = incoming[None]
    carry_mask = (stretch_ids == prior_ids[:, None]).astype(jnp.float32)
    carry_decay = jnp.exp(log_decay) * carry_mask[:, :, None]
    from_before = (
        jnp.einsum(
            "cln,chpn->clhp",
            read_state,
            arriving.astype(jnp.bfloat16),
            preferred_element_type=jnp.float32,
        )
        * carry_decay[:, :, :, None]
    )
    result = (
        within_stretch + from_before + skip_gain[None, None, :, None] * values.astype(jnp.float32)
    )
    ssm_rows = result.reshape(block_rows, local_width).astype(jnp.bfloat16)
    end_weight = ends_mask.astype(jnp.float32)
    has_end = jnp.sum(end_weight, axis=1)
    end_decay = jnp.sum(decay_heads * end_weight[:, None, :], axis=2)
    end_ids = jnp.sum(jnp.where(ends_mask, stretch_ids, 0), axis=1)
    keep_end = ((stretch_ids == end_ids[:, None]) & (has_end[:, None] > 0))[:, None, :]
    end_coef = (
        jnp.where(keep_end, jnp.exp(jnp.minimum(end_decay[:, :, None] - decay_heads, 0.0)), 0.0)
        * step_heads
    )
    end_rows = (values.astype(jnp.float32) * jnp.swapaxes(end_coef, 1, 2)[:, :, :, None]).astype(
        jnp.bfloat16
    )
    end_states = jnp.einsum(
        "clhp,cln->chpn", end_rows, write_state, preferred_element_type=jnp.float32
    )
    end_carry = (
        jnp.exp(end_decay) * ((end_ids == prior_ids) & (has_end > 0)).astype(jnp.float32)[:, None]
    )
    end_states = end_states + end_carry[:, :, None, None] * arriving
    final_block = jnp.sum(end_states, axis=0)[None]
    y_tokens = lax.all_to_all(
        ssm_rows.reshape(groups, sub_rows, local_width), "head", 0, 2, tiled=True
    ).reshape(sub_rows, inner_width)
    token_rows = (y_tokens.astype(jnp.float32), gates_tokens.astype(jnp.float32))
    gated = token_rows[0] * jax.nn.silu(token_rows[1])
    mean_square = jnp.mean(gated * gated, axis=1)
    scaled = gated * lax.rsqrt(mean_square + epsilon)[:, None] * norm_gain[None, :]
    gated_out = scaled.astype(jnp.bfloat16)
    return (gated_out, final_block)


def solution(mesh):
    seq_size, head_size = mesh.devices.shape
    fine = Mesh(mesh.devices.reshape(4, seq_size // 8, 2, head_size), SEQ + ("head",))
    in_specs = (
        P(SEQ + ("head",), None),
        P(SEQ, "head"),
        P(SEQ, "head"),
        P(SEQ, "head"),
        P(SEQ, None),
        P(),
        P(),
        P("head"),
        P("head"),
        P("head"),
        P(),
        P(),
    )
    out_specs = (P(SEQ + ("head",), None), P(SEQ, "head", None, None))
    return jax.shard_map(
        on_device, mesh=fine, in_specs=in_specs, out_specs=out_specs, check_vma=False
    )
```

```python
import jax
import jax.numpy as jnp
from jax import lax
from jax.sharding import Mesh, PartitionSpec as P

STRETCH = 256
SEQ = ("x", "z", "c")


epsilon = 1e-05


def from_behind(block, axis, distance):
    devices = range(lax.psum(1, axis))
    route = [(i - distance, i) for i in devices if i - distance in devices]
    return lax.ppermute(block, axis, route)


def segments_at(positions, prompt_ends):
    counted = jnp.sum((prompt_ends[None, :] <= positions[:, None]).astype(jnp.int32), axis=1)
    return jnp.where(positions < 0, -1, counted)


def on_device(
    hidden,
    w_values,
    w_gates,
    w_steps,
    w_states,
    conv_weight,
    conv_bias,
    step_bias,
    decay_rate,
    skip_gain,
    norm_gain,
    lengths,
):
    groups = lax.axis_size("head")
    group_index = lax.axis_index("head")
    block_index = lax.axis_index(SEQ)
    local_width = w_values.shape[1]
    inner_width = local_width * groups
    local_heads = decay_rate.shape[0]
    head_width = local_width // local_heads
    state_width = w_states.shape[1] // 2
    conv_taps = conv_weight.shape[0]
    prompt_ends = jnp.cumsum(lengths)
    block_hidden = lax.all_to_all(
        jnp.broadcast_to(hidden[None], (groups,) + hidden.shape), "head", 0, 0, tiled=True
    ).reshape(groups * hidden.shape[0], hidden.shape[1])
    block_rows = block_hidden.shape[0]
    sub_rows = block_rows // groups
    step_width = w_steps.shape[1]
    merged = jnp.concatenate([w_values, w_states, w_gates, w_steps], axis=1)
    shard_rows = merged.shape[0]
    padded_rows = -(-shard_rows // 16) * 16
    half = local_width + 2 * state_width
    merged = jnp.pad(merged, ((0, padded_rows - shard_rows), (0, 2 * half - merged.shape[1])))
    halves = jnp.stack([merged[:, :half], merged[:, half:]])
    own_half = lax.all_to_all(halves, "c", 0, 0, tiled=True).reshape(2 * padded_rows, half)
    own_half = lax.all_gather(own_half, "x", axis=0, tiled=True)
    early_start = block_index * block_rows
    ext_positions = (
        early_start - (conv_taps - 1) + jnp.arange(block_rows + conv_taps - 1, dtype=jnp.int32)
    )
    positions = early_start + jnp.arange(block_rows, dtype=jnp.int32)
    early_ids = (
        segments_at(ext_positions, prompt_ends),
        segments_at(positions, prompt_ends),
        segments_at(positions + 1, prompt_ends),
        segments_at(positions - 1, prompt_ends),
    )
    block_hidden, own_half, early_ids = lax.optimization_barrier((block_hidden, own_half, early_ids))
    ext_ids, segment_ids, next_ids, before_ids = early_ids
    own_half = lax.all_gather(own_half, "z", axis=0, tiled=True)
    other_half = lax.ppermute(own_half, "c", [(0, 1), (1, 0)])
    x_size = lax.psum(1, "x")
    z_size = lax.psum(1, "z")
    c_size = lax.psum(1, "c")
    core_index = lax.axis_index("c")

    def spread_rows(rows):
        count = rows.shape[0]
        split = rows.reshape(count, x_size, z_size, c_size, shard_rows)
        split = jnp.pad(split, ((0, 0), (0, 0), (0, 0), (0, 0), (0, padded_rows - shard_rows)))
        split = jnp.transpose(split, (0, 2, 1, 3, 4))
        return split.reshape(count, x_size * z_size * c_size * padded_rows)

    rim_hidden = from_behind(block_hidden[block_rows - (conv_taps - 1) :], SEQ, 1)
    rim_count = rim_hidden.shape[0]
    both_rows = jnp.concatenate(
        [block_hidden, rim_hidden, jnp.zeros((8 - rim_count, block_hidden.shape[1]), jnp.bfloat16)]
    )
    spread = spread_rows(both_rows)
    with_own = jnp.dot(spread, own_half, preferred_element_type=jnp.float32)
    with_other = jnp.dot(spread, other_half, preferred_element_type=jnp.float32)
    projected = jnp.zeros((with_own.shape[0], 2 * half), jnp.float32)
    projected = lax.dynamic_update_slice_in_dim(projected, with_own, core_index * half, 1)
    projected = lax.dynamic_update_slice_in_dim(projected, with_other, (1 - core_index) * half, 1)
    conv_end = local_width + 2 * state_width
    prior_rim = projected[block_rows : block_rows + rim_count, :conv_end].astype(jnp.bfloat16)
    projected = projected[:block_rows]
    pre_rows = projected[:, :conv_end].astype(jnp.bfloat16)
    gates_sum = projected[:, conv_end : conv_end + local_width]
    steps_sum = projected[:, conv_end + local_width : conv_end + local_width + step_width]
    head_gates = gates_sum.astype(jnp.bfloat16)
    gates_tokens = lax.all_to_all(
        head_gates.reshape(groups, sub_rows, local_width), "head", 0, 2, tiled=True
    ).reshape(sub_rows, inner_width)
    local_taps = jnp.concatenate(
        [
            lax.dynamic_slice_in_dim(conv_weight, group_index * local_width, local_width, 1),
            conv_weight[:, inner_width:],
        ],
        axis=1,
    )
    local_bias = jnp.concatenate(
        [
            lax.dynamic_slice_in_dim(conv_bias, group_index * local_width, local_width, 0),
            conv_bias[inner_width:],
        ],
        axis=0,
    )
    block_start = block_index * block_rows
    extended = jnp.concatenate([prior_rim, pre_rows], axis=0)
    own_ids = ext_ids[conv_taps - 1 :]
    filtered = jnp.zeros(pre_rows.shape, jnp.float32) + local_bias[None, :]
    for offset in range(conv_taps):
        matches = (ext_ids[offset : offset + block_rows] == own_ids).astype(jnp.float32)
        filtered = (
            filtered
            + local_taps[offset][None, :]
            * extended[offset : offset + block_rows].astype(jnp.float32)
            * matches[:, None]
        )
    conv_out = jax.nn.silu(filtered).astype(jnp.bfloat16)
    head_values = conv_out[:, :local_width]
    both_states = conv_out[:, local_width:]
    stretch_rows = STRETCH
    stretches = block_rows // stretch_rows
    stretch_ids = segment_ids.reshape(stretches, stretch_rows)
    prior_ids = before_ids.reshape(stretches, stretch_rows)[:, 0]
    ends_mask = (segment_ids != next_ids).reshape(stretches, stretch_rows)
    step_sizes = jax.nn.softplus(steps_sum + step_bias[None, :])
    decay_steps = step_sizes * decay_rate[None, :]
    log_decay = -jnp.cumsum(decay_steps.reshape(stretches, stretch_rows, local_heads), axis=1)
    decay_heads = jnp.swapaxes(log_decay, 1, 2)
    step_heads = jnp.swapaxes(step_sizes.reshape(stretches, stretch_rows, local_heads), 1, 2)
    values = head_values.reshape(stretches, stretch_rows, local_heads, head_width)
    write_state = both_states[:, :state_width].reshape(stretches, stretch_rows, state_width)
    read_state = both_states[:, state_width:].reshape(stretches, stretch_rows, state_width)
    intersection = jnp.einsum(
        "ctn,csn->cts", read_state, write_state, preferred_element_type=jnp.float32
    )
    token_order = jnp.arange(stretch_rows, dtype=jnp.int32)
    causal = token_order[:, None] >= token_order[None, :]
    allowed = causal[None] & (stretch_ids[:, :, None] == stretch_ids[:, None, :])
    spread = decay_heads[:, :, :, None] - decay_heads[:, :, None, :]
    weights = (
        jnp.where(allowed[:, None], jnp.exp(jnp.minimum(spread, 0.0)), 0.0)
        * step_heads[:, :, None, :]
    )
    scores = (intersection[:, None] * weights).astype(jnp.bfloat16)
    within_stretch = jnp.einsum(
        "chts,cshp->cthp", scores, values, preferred_element_type=jnp.float32
    )
    last_ids = stretch_ids[:, -1]
    tail_decay = decay_heads[:, :, -1:]
    keep_tail = (stretch_ids == last_ids[:, None])[:, None, :]
    tail_coef = (
        jnp.where(keep_tail, jnp.exp(jnp.minimum(tail_decay - decay_heads, 0.0)), 0.0) * step_heads
    )
    tail_rows = (values.astype(jnp.float32) * jnp.swapaxes(tail_coef, 1, 2)[:, :, :, None]).astype(
        jnp.bfloat16
    )
    stretch_states = jnp.einsum(
        "clhp,cln->chpn", tail_rows, write_state, preferred_element_type=jnp.float32
    )
    stretch_gates = (
        jnp.exp(decay_heads[:, :, -1]) * (last_ids == prior_ids).astype(jnp.float32)[:, None]
    )
    own_gate = jnp.broadcast_to(stretch_gates[0][:, None, None], (local_heads, 8, state_width))
    packed = jnp.concatenate([stretch_states[0], own_gate], axis=1).astype(jnp.bfloat16)
    p1 = from_behind(packed, SEQ, 1)
    p2 = from_behind(packed, SEQ, 2)
    p3 = from_behind(packed, SEQ, 3)
    g1 = p1[:, head_width : head_width + 1, :1]
    g2 = p2[:, head_width : head_width + 1, :1]
    p1, p2, p3, g1, g2 = (part.astype(jnp.float32) for part in (p1, p2, p3, g1, g2))
    incoming = p1[:, :head_width] + g1 * (p2[:, :head_width] + g2 * p3[:, :head_width])
    arriving = incoming[None]
    carry_mask = (stretch_ids == prior_ids[:, None]).astype(jnp.float32)
    carry_decay = jnp.exp(log_decay) * carry_mask[:, :, None]
    from_before = (
        jnp.einsum(
            "cln,chpn->clhp",
            read_state,
            arriving.astype(jnp.bfloat16),
            preferred_element_type=jnp.float32,
        )
        * carry_decay[:, :, :, None]
    )
    result = (
        within_stretch + from_before + skip_gain[None, None, :, None] * values.astype(jnp.float32)
    )
    ssm_rows = result.reshape(block_rows, local_width).astype(jnp.bfloat16)
    end_weight = ends_mask.astype(jnp.float32)
    has_end = jnp.sum(end_weight, axis=1)
    end_decay = jnp.sum(decay_heads * end_weight[:, None, :], axis=2)
    end_ids = jnp.sum(jnp.where(ends_mask, stretch_ids, 0), axis=1)
    keep_end = ((stretch_ids == end_ids[:, None]) & (has_end[:, None] > 0))[:, None, :]
    end_coef = (
        jnp.where(keep_end, jnp.exp(jnp.minimum(end_decay[:, :, None] - decay_heads, 0.0)), 0.0)
        * step_heads
    )
    end_rows = (values.astype(jnp.float32) * jnp.swapaxes(end_coef, 1, 2)[:, :, :, None]).astype(
        jnp.bfloat16
    )
    end_states = jnp.einsum(
        "clhp,cln->chpn", end_rows, write_state, preferred_element_type=jnp.float32
    )
    end_carry = (
        jnp.exp(end_decay) * ((end_ids == prior_ids) & (has_end > 0)).astype(jnp.float32)[:, None]
    )
    end_states = end_states + end_carry[:, :, None, None] * arriving
    final_block = jnp.sum(end_states, axis=0)[None]
    y_tokens = lax.all_to_all(
        ssm_rows.reshape(groups, sub_rows, local_width), "head", 0, 2, tiled=True
    ).reshape(sub_rows, inner_width)
    token_rows = (y_tokens.astype(jnp.float32), gates_tokens.astype(jnp.float32))
    gated = token_rows[0] * jax.nn.silu(token_rows[1])
    mean_square = jnp.mean(gated * gated, axis=1)
    scaled = gated * lax.rsqrt(mean_square + epsilon)[:, None] * norm_gain[None, :]
    gated_out = scaled.astype(jnp.bfloat16)
    return (gated_out, final_block)


def solution(mesh):
    seq_size, head_size = mesh.devices.shape
    fine = Mesh(mesh.devices.reshape(4, seq_size // 8, 2, head_size), SEQ + ("head",))
    in_specs = (
        P(SEQ + ("head",), None),
        P(SEQ, "head"),
        P(SEQ, "head"),
        P(SEQ, "head"),
        P(SEQ, None),
        P(),
        P(),
        P("head"),
        P("head"),
        P("head"),
        P(),
        P(),
    )
    out_specs = (P(SEQ + ("head",), None), P(SEQ, "head", None, None))
    return jax.shard_map(
        on_device, mesh=fine, in_specs=in_specs, out_specs=out_specs, check_vma=False
    )
```

```python
import jax
import jax.numpy as jnp
from jax import lax
from jax.sharding import Mesh, PartitionSpec as P

STRETCH = 256
SEQ = ("x", "z", "c")


epsilon = 1e-05


def from_behind(block, axis, distance):
    devices = range(lax.psum(1, axis))
    route = [(i - distance, i) for i in devices if i - distance in devices]
    return lax.ppermute(block, axis, route)


def segments_at(positions, prompt_ends):
    counted = jnp.sum((prompt_ends[None, :] <= positions[:, None]).astype(jnp.int32), axis=1)
    return jnp.where(positions < 0, -1, counted)


def on_device(
    hidden,
    w_values,
    w_gates,
    w_steps,
    w_states,
    conv_weight,
    conv_bias,
    step_bias,
    decay_rate,
    skip_gain,
    norm_gain,
    lengths,
):
    groups = lax.axis_size("head")
    group_index = lax.axis_index("head")
    block_index = lax.axis_index(SEQ)
    local_width = w_values.shape[1]
    inner_width = local_width * groups
    local_heads = decay_rate.shape[0]
    head_width = local_width // local_heads
    state_width = w_states.shape[1] // 2
    conv_taps = conv_weight.shape[0]
    prompt_ends = jnp.cumsum(lengths)
    block_hidden = lax.all_to_all(
        jnp.broadcast_to(hidden[None], (groups,) + hidden.shape), "head", 0, 0, tiled=True
    ).reshape(groups * hidden.shape[0], hidden.shape[1])
    block_rows = block_hidden.shape[0]
    sub_rows = block_rows // groups
    step_width = w_steps.shape[1]
    merged = jnp.concatenate([w_values, w_states, w_gates, w_steps], axis=1)
    shard_rows = merged.shape[0]
    padded_rows = -(-shard_rows // 16) * 16
    half = local_width + 2 * state_width
    merged = jnp.pad(merged, ((0, padded_rows - shard_rows), (0, 2 * half - merged.shape[1])))
    halves = jnp.stack([merged[:, :half], merged[:, half:]])
    own_half = lax.all_to_all(halves, "c", 0, 0, tiled=True).reshape(2 * padded_rows, half)
    x_count = lax.psum(1, "x")
    own_half = lax.all_to_all(
        jnp.broadcast_to(own_half[None], (x_count,) + own_half.shape), "x", 0, 0, tiled=True
    ).reshape(x_count * own_half.shape[0], own_half.shape[1])
    early_start = block_index * block_rows
    ext_positions = (
        early_start - (conv_taps - 1) + jnp.arange(block_rows + conv_taps - 1, dtype=jnp.int32)
    )
    positions = early_start + jnp.arange(block_rows, dtype=jnp.int32)
    early_ids = (
        segments_at(ext_positions, prompt_ends),
        segments_at(positions, prompt_ends),
        segments_at(positions + 1, prompt_ends),
        segments_at(positions - 1, prompt_ends),
    )
    block_hidden, own_half, early_ids = lax.optimization_barrier((block_hidden, own_half, early_ids))
    ext_ids, segment_ids, next_ids, before_ids = early_ids
    own_half = lax.all_gather(own_half, "z", axis=0, tiled=True)
    other_half = lax.ppermute(own_half, "c", [(0, 1), (1, 0)])
    x_size = lax.psum(1, "x")
    z_size = lax.psum(1, "z")
    c_size = lax.psum(1, "c")
    core_index = lax.axis_index("c")

    def spread_rows(rows):
        count = rows.shape[0]
        split = rows.reshape(count, x_size, z_size, c_size, shard_rows)
        split = jnp.pad(split, ((0, 0), (0, 0), (0, 0), (0, 0), (0, padded_rows - shard_rows)))
        split = jnp.transpose(split, (0, 2, 1, 3, 4))
        return split.reshape(count, x_size * z_size * c_size * padded_rows)

    rim_hidden = from_behind(block_hidden[block_rows - (conv_taps - 1) :], SEQ, 1)
    rim_count = rim_hidden.shape[0]
    both_rows = jnp.concatenate(
        [block_hidden, rim_hidden, jnp.zeros((8 - rim_count, block_hidden.shape[1]), jnp.bfloat16)]
    )
    spread = spread_rows(both_rows)
    with_own = jnp.dot(spread, own_half, preferred_element_type=jnp.float32)
    with_other = jnp.dot(spread, other_half, preferred_element_type=jnp.float32)
    first_cols = jnp.where(core_index == 0, with_own, with_other)
    second_cols = jnp.where(core_index == 0, with_other, with_own)
    projected = jnp.concatenate([first_cols, second_cols], axis=1)
    conv_end = local_width + 2 * state_width
    prior_rim = projected[block_rows : block_rows + rim_count, :conv_end].astype(jnp.bfloat16)
    projected = projected[:block_rows]
    pre_rows = projected[:, :conv_end].astype(jnp.bfloat16)
    gates_sum = projected[:, conv_end : conv_end + local_width]
    steps_sum = projected[:, conv_end + local_width : conv_end + local_width + step_width]
    head_gates = gates_sum.astype(jnp.bfloat16)
    gates_tokens = lax.all_to_all(
        head_gates.reshape(groups, sub_rows, local_width), "head", 0, 2, tiled=True
    ).reshape(sub_rows, inner_width)
    local_taps = jnp.concatenate(
        [
            lax.dynamic_slice_in_dim(conv_weight, group_index * local_width, local_width, 1),
            conv_weight[:, inner_width:],
        ],
        axis=1,
    )
    local_bias = jnp.concatenate(
        [
            lax.dynamic_slice_in_dim(conv_bias, group_index * local_width, local_width, 0),
            conv_bias[inner_width:],
        ],
        axis=0,
    )
    block_start = block_index * block_rows
    extended = jnp.concatenate([prior_rim, pre_rows], axis=0)
    own_ids = ext_ids[conv_taps - 1 :]
    filtered = jnp.zeros(pre_rows.shape, jnp.float32) + local_bias[None, :]
    for offset in range(conv_taps):
        matches = (ext_ids[offset : offset + block_rows] == own_ids).astype(jnp.float32)
        filtered = (
            filtered
            + local_taps[offset][None, :]
            * extended[offset : offset + block_rows].astype(jnp.float32)
            * matches[:, None]
        )
    conv_out = jax.nn.silu(filtered).astype(jnp.bfloat16)
    head_values = conv_out[:, :local_width]
    both_states = conv_out[:, local_width:]
    stretch_rows = STRETCH
    stretches = block_rows // stretch_rows
    stretch_ids = segment_ids.reshape(stretches, stretch_rows)
    prior_ids = before_ids.reshape(stretches, stretch_rows)[:, 0]
    ends_mask = (segment_ids != next_ids).reshape(stretches, stretch_rows)
    step_sizes = jax.nn.softplus(steps_sum + step_bias[None, :])
    decay_steps = step_sizes * decay_rate[None, :]
    log_decay = -jnp.cumsum(decay_steps.reshape(stretches, stretch_rows, local_heads), axis=1)
    decay_heads = jnp.swapaxes(log_decay, 1, 2)
    step_heads = jnp.swapaxes(step_sizes.reshape(stretches, stretch_rows, local_heads), 1, 2)
    values = head_values.reshape(stretches, stretch_rows, local_heads, head_width)
    write_state = both_states[:, :state_width].reshape(stretches, stretch_rows, state_width)
    read_state = both_states[:, state_width:].reshape(stretches, stretch_rows, state_width)
    intersection = jnp.einsum(
        "ctn,csn->cts", read_state, write_state, preferred_element_type=jnp.float32
    )
    token_order = jnp.arange(stretch_rows, dtype=jnp.int32)
    causal = token_order[:, None] >= token_order[None, :]
    allowed = causal[None] & (stretch_ids[:, :, None] == stretch_ids[:, None, :])
    spread = decay_heads[:, :, :, None] - decay_heads[:, :, None, :]
    weights = (
        jnp.where(allowed[:, None], jnp.exp(jnp.minimum(spread, 0.0)), 0.0)
        * step_heads[:, :, None, :]
    )
    scores = (intersection[:, None] * weights).astype(jnp.bfloat16)
    within_stretch = jnp.einsum(
        "chts,cshp->cthp", scores, values, preferred_element_type=jnp.float32
    )
    last_ids = stretch_ids[:, -1]
    tail_decay = decay_heads[:, :, -1:]
    keep_tail = (stretch_ids == last_ids[:, None])[:, None, :]
    tail_coef = (
        jnp.where(keep_tail, jnp.exp(jnp.minimum(tail_decay - decay_heads, 0.0)), 0.0) * step_heads
    )
    tail_rows = (values.astype(jnp.float32) * jnp.swapaxes(tail_coef, 1, 2)[:, :, :, None]).astype(
        jnp.bfloat16
    )
    stretch_states = jnp.einsum(
        "clhp,cln->chpn", tail_rows, write_state, preferred_element_type=jnp.float32
    )
    stretch_gates = (
        jnp.exp(decay_heads[:, :, -1]) * (last_ids == prior_ids).astype(jnp.float32)[:, None]
    )
    own_gate = jnp.broadcast_to(stretch_gates[0][:, None, None], (local_heads, 8, state_width))
    packed = jnp.concatenate([stretch_states[0], own_gate], axis=1).astype(jnp.bfloat16)
    p1 = from_behind(packed, SEQ, 1)
    p2 = from_behind(packed, SEQ, 2)
    p3 = from_behind(packed, SEQ, 3)
    g1 = p1[:, head_width : head_width + 1, :1]
    g2 = p2[:, head_width : head_width + 1, :1]
    p1, p2, p3, g1, g2 = (part.astype(jnp.float32) for part in (p1, p2, p3, g1, g2))
    incoming = p1[:, :head_width] + g1 * (p2[:, :head_width] + g2 * p3[:, :head_width])
    arriving = incoming[None]
    carry_mask = (stretch_ids == prior_ids[:, None]).astype(jnp.float32)
    carry_decay = jnp.exp(log_decay) * carry_mask[:, :, None]
    from_before = (
        jnp.einsum(
            "cln,chpn->clhp",
            read_state,
            arriving.astype(jnp.bfloat16),
            preferred_element_type=jnp.float32,
        )
        * carry_decay[:, :, :, None]
    )
    result = (
        within_stretch + from_before + skip_gain[None, None, :, None] * values.astype(jnp.float32)
    )
    ssm_rows = result.reshape(block_rows, local_width).astype(jnp.bfloat16)
    end_weight = ends_mask.astype(jnp.float32)
    has_end = jnp.sum(end_weight, axis=1)
    end_decay = jnp.sum(decay_heads * end_weight[:, None, :], axis=2)
    end_ids = jnp.sum(jnp.where(ends_mask, stretch_ids, 0), axis=1)
    keep_end = ((stretch_ids == end_ids[:, None]) & (has_end[:, None] > 0))[:, None, :]
    end_coef = (
        jnp.where(keep_end, jnp.exp(jnp.minimum(end_decay[:, :, None] - decay_heads, 0.0)), 0.0)
        * step_heads
    )
    end_rows = (values.astype(jnp.float32) * jnp.swapaxes(end_coef, 1, 2)[:, :, :, None]).astype(
        jnp.bfloat16
    )
    end_states = jnp.einsum(
        "clhp,cln->chpn", end_rows, write_state, preferred_element_type=jnp.float32
    )
    end_carry = (
        jnp.exp(end_decay) * ((end_ids == prior_ids) & (has_end > 0)).astype(jnp.float32)[:, None]
    )
    end_states = end_states + end_carry[:, :, None, None] * arriving
    final_block = jnp.sum(end_states, axis=0)[None]
    y_tokens = lax.all_to_all(
        ssm_rows.reshape(groups, sub_rows, local_width), "head", 0, 2, tiled=True
    ).reshape(sub_rows, inner_width)
    token_rows = (y_tokens.astype(jnp.float32), gates_tokens.astype(jnp.float32))
    gated = token_rows[0] * jax.nn.silu(token_rows[1])
    mean_square = jnp.mean(gated * gated, axis=1)
    scaled = gated * lax.rsqrt(mean_square + epsilon)[:, None] * norm_gain[None, :]
    gated_out = scaled.astype(jnp.bfloat16)
    return (gated_out, final_block)


def solution(mesh):
    seq_size, head_size = mesh.devices.shape
    fine = Mesh(mesh.devices.reshape(4, seq_size // 8, 2, head_size), SEQ + ("head",))
    in_specs = (
        P(SEQ + ("head",), None),
        P(SEQ, "head"),
        P(SEQ, "head"),
        P(SEQ, "head"),
        P(SEQ, None),
        P(),
        P(),
        P("head"),
        P("head"),
        P("head"),
        P(),
        P(),
    )
    out_specs = (P(SEQ + ("head",), None), P(SEQ, "head", None, None))
    return jax.shard_map(
        on_device, mesh=fine, in_specs=in_specs, out_specs=out_specs, check_vma=False
    )
```

```python
import jax
import jax.numpy as jnp
from jax import lax
from jax.sharding import Mesh, PartitionSpec as P

STRETCH = 256
SEQ = ("x", "z", "c")


epsilon = 1e-05


def from_behind(block, axis, distance):
    devices = range(lax.psum(1, axis))
    route = [(i - distance, i) for i in devices if i - distance in devices]
    return lax.ppermute(block, axis, route)


def segments_at(positions, prompt_ends):
    counted = jnp.sum((prompt_ends[None, :] <= positions[:, None]).astype(jnp.int32), axis=1)
    return jnp.where(positions < 0, -1, counted)


def on_device(
    hidden,
    w_values,
    w_gates,
    w_steps,
    w_states,
    conv_weight,
    conv_bias,
    step_bias,
    decay_rate,
    skip_gain,
    norm_gain,
    lengths,
):
    groups = lax.axis_size("head")
    group_index = lax.axis_index("head")
    block_index = lax.axis_index(SEQ)
    local_width = w_values.shape[1]
    inner_width = local_width * groups
    local_heads = decay_rate.shape[0]
    head_width = local_width // local_heads
    state_width = w_states.shape[1] // 2
    conv_taps = conv_weight.shape[0]
    prompt_ends = jnp.cumsum(lengths)
    block_hidden = lax.all_to_all(
        jnp.broadcast_to(hidden[None], (groups,) + hidden.shape), "head", 0, 0, tiled=True
    ).reshape(groups * hidden.shape[0], hidden.shape[1])
    block_rows = block_hidden.shape[0]
    sub_rows = block_rows // groups
    step_width = w_steps.shape[1]
    merged = jnp.concatenate([w_values, w_states, w_gates, w_steps], axis=1)
    shard_rows = merged.shape[0]
    padded_rows = -(-shard_rows // 16) * 16
    half = local_width + 2 * state_width
    merged = jnp.pad(merged, ((0, padded_rows - shard_rows), (0, 2 * half - merged.shape[1])))
    halves = jnp.stack([merged[:, :half], merged[:, half:]])
    own_half = lax.all_to_all(halves, "c", 0, 0, tiled=True).reshape(2 * padded_rows, half)
    own_half = lax.all_gather(own_half, "x", axis=0, tiled=True)
    early_start = block_index * block_rows
    ext_positions = (
        early_start - (conv_taps - 1) + jnp.arange(block_rows + conv_taps - 1, dtype=jnp.int32)
    )
    positions = early_start + jnp.arange(block_rows, dtype=jnp.int32)
    early_ids = (
        segments_at(ext_positions, prompt_ends),
        segments_at(positions, prompt_ends),
        segments_at(positions + 1, prompt_ends),
        segments_at(positions - 1, prompt_ends),
    )
    block_hidden, own_half, early_ids = lax.optimization_barrier((block_hidden, own_half, early_ids))
    ext_ids, segment_ids, next_ids, before_ids = early_ids
    own_half = lax.all_gather(own_half, "z", axis=0, tiled=True)
    other_half = lax.ppermute(own_half, "c", [(0, 1), (1, 0)])
    x_size = lax.psum(1, "x")
    z_size = lax.psum(1, "z")
    c_size = lax.psum(1, "c")
    core_index = lax.axis_index("c")

    def spread_rows(rows):
        count = rows.shape[0]
        split = rows.reshape(count, x_size, z_size, c_size, shard_rows)
        split = jnp.pad(split, ((0, 0), (0, 0), (0, 0), (0, 0), (0, padded_rows - shard_rows)))
        split = jnp.transpose(split, (0, 2, 1, 3, 4))
        return split.reshape(count, x_size * z_size * c_size * padded_rows)

    rim_hidden = from_behind(block_hidden[block_rows - (conv_taps - 1) :], SEQ, 1)
    rim_count = rim_hidden.shape[0]
    both_rows = jnp.concatenate(
        [block_hidden, rim_hidden, jnp.zeros((8 - rim_count, block_hidden.shape[1]), jnp.bfloat16)]
    )
    spread = spread_rows(both_rows)
    with_own = jnp.dot(spread, own_half, preferred_element_type=jnp.float32)
    with_other = jnp.dot(spread, other_half, preferred_element_type=jnp.float32)
    first_cols = jnp.where(core_index == 0, with_own, with_other)
    second_cols = jnp.where(core_index == 0, with_other, with_own)
    projected = jnp.concatenate([first_cols, second_cols], axis=1)
    conv_end = local_width + 2 * state_width
    prior_rim = projected[block_rows : block_rows + rim_count, :conv_end].astype(jnp.bfloat16)
    projected = projected[:block_rows]
    pre_rows = projected[:, :conv_end].astype(jnp.bfloat16)
    gates_sum = projected[:, conv_end : conv_end + local_width]
    steps_sum = projected[:, conv_end + local_width : conv_end + local_width + step_width]
    head_gates = gates_sum.astype(jnp.bfloat16)
    local_taps = jnp.concatenate(
        [
            lax.dynamic_slice_in_dim(conv_weight, group_index * local_width, local_width, 1),
            conv_weight[:, inner_width:],
        ],
        axis=1,
    )
    local_bias = jnp.concatenate(
        [
            lax.dynamic_slice_in_dim(conv_bias, group_index * local_width, local_width, 0),
            conv_bias[inner_width:],
        ],
        axis=0,
    )
    block_start = block_index * block_rows
    extended = jnp.concatenate([prior_rim, pre_rows], axis=0)
    own_ids = ext_ids[conv_taps - 1 :]
    filtered = jnp.zeros(pre_rows.shape, jnp.float32) + local_bias[None, :]
    for offset in range(conv_taps):
        matches = (ext_ids[offset : offset + block_rows] == own_ids).astype(jnp.float32)
        filtered = (
            filtered
            + local_taps[offset][None, :]
            * extended[offset : offset + block_rows].astype(jnp.float32)
            * matches[:, None]
        )
    conv_out = jax.nn.silu(filtered).astype(jnp.bfloat16)
    head_values = conv_out[:, :local_width]
    both_states = conv_out[:, local_width:]
    stretch_rows = STRETCH
    stretches = block_rows // stretch_rows
    stretch_ids = segment_ids.reshape(stretches, stretch_rows)
    prior_ids = before_ids.reshape(stretches, stretch_rows)[:, 0]
    ends_mask = (segment_ids != next_ids).reshape(stretches, stretch_rows)
    step_sizes = jax.nn.softplus(steps_sum + step_bias[None, :])
    decay_steps = step_sizes * decay_rate[None, :]
    log_decay = -jnp.cumsum(decay_steps.reshape(stretches, stretch_rows, local_heads), axis=1)
    decay_heads = jnp.swapaxes(log_decay, 1, 2)
    step_heads = jnp.swapaxes(step_sizes.reshape(stretches, stretch_rows, local_heads), 1, 2)
    values = head_values.reshape(stretches, stretch_rows, local_heads, head_width)
    write_state = both_states[:, :state_width].reshape(stretches, stretch_rows, state_width)
    read_state = both_states[:, state_width:].reshape(stretches, stretch_rows, state_width)
    intersection = jnp.einsum(
        "ctn,csn->cts", read_state, write_state, preferred_element_type=jnp.float32
    )
    token_order = jnp.arange(stretch_rows, dtype=jnp.int32)
    causal = token_order[:, None] >= token_order[None, :]
    allowed = causal[None] & (stretch_ids[:, :, None] == stretch_ids[:, None, :])
    spread = decay_heads[:, :, :, None] - decay_heads[:, :, None, :]
    weights = (
        jnp.where(allowed[:, None], jnp.exp(jnp.minimum(spread, 0.0)), 0.0)
        * step_heads[:, :, None, :]
    )
    scores = (intersection[:, None] * weights).astype(jnp.bfloat16)
    within_stretch = jnp.einsum(
        "chts,cshp->cthp", scores, values, preferred_element_type=jnp.float32
    )
    last_ids = stretch_ids[:, -1]
    tail_decay = decay_heads[:, :, -1:]
    keep_tail = (stretch_ids == last_ids[:, None])[:, None, :]
    tail_coef = (
        jnp.where(keep_tail, jnp.exp(jnp.minimum(tail_decay - decay_heads, 0.0)), 0.0) * step_heads
    )
    tail_rows = (values.astype(jnp.float32) * jnp.swapaxes(tail_coef, 1, 2)[:, :, :, None]).astype(
        jnp.bfloat16
    )
    stretch_states = jnp.einsum(
        "clhp,cln->chpn", tail_rows, write_state, preferred_element_type=jnp.float32
    )
    stretch_gates = (
        jnp.exp(decay_heads[:, :, -1]) * (last_ids == prior_ids).astype(jnp.float32)[:, None]
    )
    own_gate = jnp.broadcast_to(stretch_gates[0][:, None, None], (local_heads, 8, state_width))
    packed = jnp.concatenate([stretch_states[0], own_gate], axis=1).astype(jnp.bfloat16)
    p1 = from_behind(packed, SEQ, 1)
    p2 = from_behind(packed, SEQ, 2)
    p3 = from_behind(packed, SEQ, 3)
    g1 = p1[:, head_width : head_width + 1, :1]
    g2 = p2[:, head_width : head_width + 1, :1]
    p1, p2, p3, g1, g2 = (part.astype(jnp.float32) for part in (p1, p2, p3, g1, g2))
    incoming = p1[:, :head_width] + g1 * (p2[:, :head_width] + g2 * p3[:, :head_width])
    arriving = incoming[None]
    carry_mask = (stretch_ids == prior_ids[:, None]).astype(jnp.float32)
    carry_decay = jnp.exp(log_decay) * carry_mask[:, :, None]
    from_before = (
        jnp.einsum(
            "cln,chpn->clhp",
            read_state,
            arriving.astype(jnp.bfloat16),
            preferred_element_type=jnp.float32,
        )
        * carry_decay[:, :, :, None]
    )
    result = (
        within_stretch + from_before + skip_gain[None, None, :, None] * values.astype(jnp.float32)
    )
    ssm_rows = result.reshape(block_rows, local_width).astype(jnp.bfloat16)
    end_weight = ends_mask.astype(jnp.float32)
    has_end = jnp.sum(end_weight, axis=1)
    end_decay = jnp.sum(decay_heads * end_weight[:, None, :], axis=2)
    end_ids = jnp.sum(jnp.where(ends_mask, stretch_ids, 0), axis=1)
    keep_end = ((stretch_ids == end_ids[:, None]) & (has_end[:, None] > 0))[:, None, :]
    end_coef = (
        jnp.where(keep_end, jnp.exp(jnp.minimum(end_decay[:, :, None] - decay_heads, 0.0)), 0.0)
        * step_heads
    )
    end_rows = (values.astype(jnp.float32) * jnp.swapaxes(end_coef, 1, 2)[:, :, :, None]).astype(
        jnp.bfloat16
    )
    end_states = jnp.einsum(
        "clhp,cln->chpn", end_rows, write_state, preferred_element_type=jnp.float32
    )
    end_carry = (
        jnp.exp(end_decay) * ((end_ids == prior_ids) & (has_end > 0)).astype(jnp.float32)[:, None]
    )
    end_states = end_states + end_carry[:, :, None, None] * arriving
    final_block = jnp.sum(end_states, axis=0)[None]
    both = jnp.stack([ssm_rows, head_gates]).reshape(2, groups, sub_rows, local_width)
    returned = lax.all_to_all(both, "head", split_axis=1, concat_axis=3, tiled=True)
    token_rows = returned.reshape(2, sub_rows, inner_width).astype(jnp.float32)
    gated = token_rows[0] * jax.nn.silu(token_rows[1])
    mean_square = jnp.mean(gated * gated, axis=1)
    scaled = gated * lax.rsqrt(mean_square + epsilon)[:, None] * norm_gain[None, :]
    gated_out = scaled.astype(jnp.bfloat16)
    return (gated_out, final_block)


def solution(mesh):
    seq_size, head_size = mesh.devices.shape
    fine = Mesh(mesh.devices.reshape(4, seq_size // 8, 2, head_size), SEQ + ("head",))
    in_specs = (
        P(SEQ + ("head",), None),
        P(SEQ, "head"),
        P(SEQ, "head"),
        P(SEQ, "head"),
        P(SEQ, None),
        P(),
        P(),
        P("head"),
        P("head"),
        P("head"),
        P(),
        P(),
    )
    out_specs = (P(SEQ + ("head",), None), P(SEQ, "head", None, None))
    return jax.shard_map(
        on_device, mesh=fine, in_specs=in_specs, out_specs=out_specs, check_vma=False
    )
```
